512 devices in a mesh: ctx: 32 (over z, x), exp: 16 (over y, core).
Axes of the slice: x: 4, y: 8, z: 8, core: 2. Of those that a mesh axis runs over, the one named last changes fastest.
Arguments:
- stream: bfloat16 [16, 4096, 1024], P('exp', 'ctx'), may hold values from -400 to 400
- queries: bfloat16 [16, 4096, 16, 128], P('exp', 'ctx'), may hold values from -6 to 6
- key_rows: bfloat16 [16, 4096, 2, 128], P('exp', 'ctx'), may hold values from -4 to 4
- value_rows: bfloat16 [16, 4096, 2, 128], P('exp', 'ctx'), may hold values from -6 to 6
- expert_ids: int32 [16, 4096, 2], P('exp', 'ctx'), may hold values from 0 to 127, as said below
- norm_gain: bfloat16 [1024], replicated, may hold values from 0.099609375 to 1.8984375
- router_weight: bfloat16 [1024, 128], replicated, may hold values from -0.1875 to 0.1875
- gate_weight: bfloat16 [98304, 1024], P(('ctx', 'exp')), may hold values from -0.1875 to 0.1875
- up_weight: bfloat16 [98304, 1024], P(('ctx', 'exp')), may hold values from -0.1875 to 0.1875
- down_weight: bfloat16 [98304, 1024], P(('ctx', 'exp')), may hold values from -0.21875 to 0.21875
Outputs:
- attended: bfloat16 [16, 4096, 16, 128], P('exp', 'ctx')
- expert_mix: bfloat16 [16, 4096, 1024], P('exp', 'ctx')
The draws below stay inside these ranges and needn't reach their ends.
Inputs may be any that keep to these rules, and one draw needn't show every extreme that they name: `expert_ids`: within the rows of one device (aligned blocks of 128 positions of one sequence), a token's 2 experts differ and no expert is named more than 4 times; one expert is named exactly 4 times in every such block.
All inputs are finite; a program needn't handle non-finite values.
Results may differ from the reference program's by a relative error of at most 0.01.
Values may be sent and summed in bfloat16 or wider, within the bound.
No kernel may reach another device: no remote copies, remote signals or barrier semaphores. Data moves between devices by JAX's collectives and lax.ppermute only.
A program may use at most 64 MiB of HBM per device.

```python
import math
import jax
import jax.numpy as jnp
from jax import lax

D = 1024
HEADS = 16
KV_HEADS = 2
HEAD_DIM = 128
FF = 768
TOP = 2
TOK_DEV = 128
BATCH = 16
SEQ = 4096
EXPERTS = 128
CAP = 4
N_CTX = 32
N_EXP = 16


def draw_stream(key, part):
    noise_key, row_key, column_key = jax.random.split(jax.random.fold_in(key, 21), 3)
    noise_field = jnp.clip(jax.random.normal(noise_key, (BATCH, SEQ, D), jnp.float32), -4.0, 4.0)
    columns = jnp.exp(jax.random.uniform(column_key, (D,), jnp.float32, 0.0, math.log(10.0)))
    row_scale = jnp.exp(jax.random.uniform(row_key, (BATCH, SEQ, 1), jnp.float32, 0.0, math.log(10.0)))
    return (noise_field * row_scale * columns).astype(jnp.bfloat16)


def draw_queries(key, part):
    noise_key = jax.random.fold_in(key, 11)
    shape_all = (BATCH, SEQ, HEADS, HEAD_DIM)
    return jnp.clip(jax.random.normal(noise_key, shape_all, jnp.float32), -4.0, 4.0).astype(jnp.bfloat16)


def draw_key_rows(key, part):
    noise_key = jax.random.fold_in(key, 13)
    shape_all = (BATCH, SEQ, KV_HEADS, HEAD_DIM)
    return jnp.clip(jax.random.normal(noise_key, shape_all, jnp.float32), -4.0, 4.0).astype(jnp.bfloat16)


def draw_expert_ids(key, part):
    block_total = BATCH * (SEQ // TOK_DEV)
    favoured = jax.random.randint(jax.random.fold_in(key, 99), (), 0, EXPERTS)

    def one_block(block_key):
        order_key, count_key, row_key = jax.random.split(block_key, 3)
        ordering = jax.random.permutation(order_key, EXPERTS)
        shares = jax.random.randint(count_key, (EXPERTS // 2,), 0, CAP + 1)
        counts = jnp.zeros((EXPERTS,), jnp.int32).at[ordering[0::2]].set(shares).at[ordering[1::2]].set(CAP - shares)
        where_fav = jnp.argmax((ordering == favoured).astype(jnp.int32))
        partner = ordering[jnp.bitwise_xor(where_fav, 1)]
        counts = counts.at[partner].set(0).at[favoured].set(CAP)
        tickets = jnp.repeat(jnp.arange(EXPERTS, dtype=jnp.int32), counts, total_repeat_length=TOK_DEV * TOP)
        ticket_table = tickets.reshape(TOP, TOK_DEV).T
        shuffle = jax.random.permutation(row_key, TOK_DEV)
        return ticket_table[shuffle]
    blocks = jax.vmap(one_block)(jax.random.split(jax.random.fold_in(key, 5), block_total))
    return blocks.reshape(BATCH, SEQ, TOP).astype(jnp.int32)


def block_levels(own_key, shape, cuts, smallest, high):
    def one(dim, shards_of):
        draws = jax.random.uniform(jax.random.fold_in(jax.random.fold_in(own_key, 6), dim), (shards_of,), jnp.float32, smallest / len(cuts), high / len(cuts))
        return jnp.repeat(jnp.exp(draws), shape[dim] // shards_of).reshape((-1,) + (1,) * (len(shape) - dim - 1))

    gain = one(*cuts[0])
    for cut in cuts[1:]:
        gain = gain * one(*cut)
    return gain


def normal_values(own_key, shape, deviation, most, shards=(), kind=jnp.bfloat16):
    loudness = block_levels(own_key, shape, shards, -0.22, 0.18) if shards else 1.0
    drawn = jax.random.normal(own_key, shape, jnp.float32) * deviation * loudness
    return jnp.minimum(jnp.maximum(drawn, -most), most).astype(kind)


def setup_inputs(seed: int = 0) -> dict:
    key_of = jax.random.split(jax.random.key(seed), 11)
    return {
        "stream": draw_stream(jax.random.fold_in(key_of[10], 71), 0),
        "queries": draw_queries(jax.random.fold_in(key_of[10], 71), 0),
        "key_rows": draw_key_rows(jax.random.fold_in(key_of[10], 71), 0),
        "value_rows": normal_values(key_of[3], (BATCH, SEQ, KV_HEADS, HEAD_DIM), 1.0, 6.0, ((0, 16), (1, 32))),
        "expert_ids": draw_expert_ids(jax.random.fold_in(key_of[10], 71), 0),
        "norm_gain": jnp.clip(1.0 + 0.18 * jax.random.normal(key_of[5], (D,), jnp.float32), 0.099609375, 1.8984375).astype(jnp.bfloat16),
        "router_weight": normal_values(key_of[6], (D, EXPERTS), D ** -0.5, 0.1875),
        "gate_weight": normal_values(key_of[7], (EXPERTS * FF, D), D ** -0.5, 0.1875, ((0, 512),)),
        "up_weight": normal_values(key_of[8], (EXPERTS * FF, D), D ** -0.5, 0.1875, ((0, 512),)),
        "down_weight": normal_values(key_of[9], (EXPERTS * FF, D), FF ** -0.5, 0.21875, ((0, 512),)),
    }


def attend_sequence(query_seq, key_seq, value_seq):
    group_size = HEADS // KV_HEADS
    scaling = 1.0 / math.sqrt(HEAD_DIM)
    block_rows = math.gcd(SEQ, 512)
    outputs = []
    for first_row in range(0, SEQ, block_rows):
        last_row = first_row + block_rows
        query_block = query_seq[first_row:last_row].reshape(block_rows, KV_HEADS, group_size, HEAD_DIM).astype(jnp.float32)
        key_block = key_seq[:last_row].astype(jnp.float32)
        value_block = value_seq[:last_row].astype(jnp.float32)
        scores = jnp.einsum('qhgd,khd->hgqk', query_block, key_block) * scaling
        key_pos = jnp.arange(last_row, dtype=jnp.int32)
        query_pos = first_row + jnp.arange(block_rows, dtype=jnp.int32)
        visible = key_pos[None, :] <= query_pos[:, None]
        scores = jnp.where(visible, scores, -jnp.inf)
        highest = lax.optimization_barrier(jnp.max(scores, axis=-1, keepdims=True))
        weights = jnp.exp(scores - highest)
        totals = lax.optimization_barrier(jnp.sum(weights, axis=-1))
        rounded = lax.optimization_barrier(weights.astype(jnp.bfloat16)).astype(jnp.float32)
        result = jnp.einsum('hgqk,khd->hgqd', rounded, value_block) / totals[..., None]
        result = jnp.transpose(result, (2, 0, 1, 3)).reshape(block_rows, HEADS, HEAD_DIM)
        outputs.append(result.astype(jnp.bfloat16))
    return jnp.concatenate(outputs, axis=0)

def reference(stream, queries, key_rows, value_rows, expert_ids, norm_gain, router_weight, gate_weight, up_weight, down_weight):
    attended = lax.map(lambda members: attend_sequence(members[0], members[1], members[2]), (queries, key_rows, value_rows))
    row_total = BATCH * SEQ
    widened = stream.astype(jnp.float32).reshape(row_total, D)
    mean_square = lax.optimization_barrier(jnp.mean(widened * widened, axis=-1, keepdims=True))
    normed = (widened * lax.rsqrt(mean_square + 1e-06) * norm_gain.astype(jnp.float32)).astype(jnp.bfloat16)
    logits = jnp.dot(normed, router_weight, preferred_element_type=jnp.float32)
    flat_ids = expert_ids.reshape(row_total, TOP).astype(jnp.int32)
    gate_values = jax.nn.sigmoid(jnp.take_along_axis(logits, flat_ids, axis=1))
    limit_rows = N_EXP * N_CTX * CAP

    def per_expert(total, expert):
        hits = flat_ids == expert
        selected = jnp.any(hits, axis=1)
        weight_here = lax.optimization_barrier(jnp.sum(jnp.where(hits, gate_values, 0.0), axis=1))
        rows_index = jnp.nonzero(selected, size=limit_rows, fill_value=0)[0].astype(jnp.int32)
        valid = jnp.arange(limit_rows, dtype=jnp.int32) < jnp.sum(selected.astype(jnp.int32))
        inputs = normed[rows_index]
        first_row = (expert * FF).astype(jnp.int32)
        gate_block = lax.dynamic_slice_in_dim(gate_weight, first_row, FF, 0)
        up_block = lax.dynamic_slice_in_dim(up_weight, first_row, FF, 0)
        down_block = lax.dynamic_slice_in_dim(down_weight, first_row, FF, 0)
        gate_part = jnp.dot(inputs, gate_block.T, preferred_element_type=jnp.float32)
        up_part = jnp.dot(inputs, up_block.T, preferred_element_type=jnp.float32)
        hidden = (jax.nn.silu(gate_part) * up_part).astype(jnp.bfloat16)
        projected = jnp.dot(hidden, down_block, preferred_element_type=jnp.float32)
        expert_out = lax.optimization_barrier(projected.astype(jnp.bfloat16)).astype(jnp.float32)
        scale_rows = jnp.where(valid, weight_here[rows_index], 0.0)
        total = total.at[rows_index].add(scale_rows[:, None] * expert_out)
        return (total, None)
    total, unused = lax.scan(per_expert, jnp.zeros((row_total, D), jnp.float32), jnp.arange(EXPERTS, dtype=jnp.int32))
    expert_mix = total.astype(jnp.bfloat16).reshape(BATCH, SEQ, D)
    return (attended, expert_mix)
```

```python
import functools
import math

import jax
import jax.numpy as jnp
from jax import lax
from jax.experimental import pallas as pl
from jax.experimental.pallas import tpu as pltpu
from jax.sharding import PartitionSpec as P


def from_partner(value, axis, flip):
    return lax.ppermute(value, axis, [(i, i ^ flip) for i in range(lax.axis_size(axis))])


def expert_rows(flat_rows, gate_rows, up_rows, down_rows):
    contract = (((1,), (1,)), ((), ()))
    gate_part = lax.dot_general(flat_rows, gate_rows, contract, preferred_element_type=jnp.float32)
    up_part = lax.dot_general(flat_rows, up_rows, contract, preferred_element_type=jnp.float32)
    hidden = (jax.nn.silu(gate_part) * up_part).astype(jnp.bfloat16)
    return jnp.dot(hidden, down_rows, preferred_element_type=jnp.float32)


def _flash_kernel(block, group, scaling, c_ref, q_ref, k_ref, v_ref, o_ref, m_sc, l_sc, acc_sc):
    c = c_ref[0]
    q = q_ref[0]
    rows = q.shape[0]
    m_sc[...] = jnp.full(m_sc.shape, -1e30, jnp.float32)
    l_sc[...] = jnp.zeros(l_sc.shape, jnp.float32)
    acc_sc[...] = jnp.zeros(acc_sc.shape, jnp.float32)

    def update(j, masked):
        start = pl.multiple_of(j * block, block)
        k = k_ref[0, pl.ds(start, block), :]
        v = v_ref[0, pl.ds(start, block), :]
        s = lax.dot_general(q, k, (((1,), (1,)), ((), ())), preferred_element_type=jnp.float32)
        s = s * scaling
        if masked:
            qpos = lax.broadcasted_iota(jnp.int32, (rows, block), 0) // group
            kpos = lax.broadcasted_iota(jnp.int32, (rows, block), 1)
            s = jnp.where(kpos <= qpos, s, -1e30)
        m_prev = m_sc[...]
        m_new = jnp.maximum(m_prev, jnp.max(s, axis=1, keepdims=True))
        alpha = jnp.exp(m_prev - m_new)
        p = jnp.exp(s - m_new)
        l_sc[...] = alpha * l_sc[...] + jnp.sum(p, axis=1, keepdims=True)
        acc_sc[...] = alpha * acc_sc[...] + jnp.dot(
            p.astype(jnp.bfloat16), v, preferred_element_type=jnp.float32
        )
        m_sc[...] = m_new

    def body(j, carry):
        update(j, False)
        return carry

    lax.fori_loop(0, c, body, 0)
    update(c, True)
    o_ref[0] = (acc_sc[...] / l_sc[...]).astype(o_ref.dtype)


def attention(queries, key_rows, value_rows):
    seq_rows = queries.shape[1]
    head_count = queries.shape[2]
    head_size = queries.shape[3]
    kv_count = key_rows.shape[2]
    group_size = head_count // kv_count
    scaling = 1.0 / math.sqrt(head_size)
    grouped = (
        queries[0]
        .reshape(seq_rows, kv_count, group_size, head_size)
        .transpose(1, 0, 2, 3)
        .reshape(kv_count, seq_rows * group_size, head_size)
    )
    keys_local = key_rows[0].transpose(1, 0, 2)
    values_local = value_rows[0].transpose(1, 0, 2)
    keys_all = lax.all_gather(keys_local, "ctx", axis=1, tiled=True)
    values_all = lax.all_gather(values_local, "ctx", axis=1, tiled=True)
    total_rows = keys_all.shape[1]
    q_rows = seq_rows * group_size
    me = lax.axis_index("ctx").astype(jnp.int32).reshape(1)
    ctx_count = lax.axis_size("ctx")
    flops = 4 * kv_count * q_rows * total_rows * head_size // 2
    out = pl.pallas_call(
        functools.partial(_flash_kernel, seq_rows, group_size, scaling),
        grid_spec=pltpu.PrefetchScalarGridSpec(
            num_scalar_prefetch=1,
            grid=(kv_count,),
            in_specs=[
                pl.BlockSpec((1, q_rows, head_size), lambda g, c: (g, 0, 0)),
                pl.BlockSpec((1, total_rows, head_size), lambda g, c: (g, 0, 0)),
                pl.BlockSpec((1, total_rows, head_size), lambda g, c: (g, 0, 0)),
            ],
            out_specs=pl.BlockSpec((1, q_rows, head_size), lambda g, c: (g, 0, 0)),
            scratch_shapes=[
                pltpu.VMEM((q_rows, 1), jnp.float32),
                pltpu.VMEM((q_rows, 1), jnp.float32),
                pltpu.VMEM((q_rows, head_size), jnp.float32),
            ],
        ),
        out_shape=jax.ShapeDtypeStruct((kv_count, q_rows, head_size), jnp.bfloat16),
        cost_estimate=pl.CostEstimate(
            flops=flops,
            transcendentals=kv_count * q_rows * total_rows // 2,
            bytes_accessed=4 * kv_count * total_rows * head_size + 4 * kv_count * q_rows * head_size,
        ),
    )(me, grouped, keys_all, values_all)
    del ctx_count
    return (
        out.reshape(kv_count, seq_rows, group_size, head_size)
        .transpose(1, 0, 2, 3)
        .reshape(1, seq_rows, head_count, head_size)
    )


def local(
    stream,
    queries,
    key_rows,
    value_rows,
    expert_ids,
    norm_gain,
    router_weight,
    gate_weight,
    up_weight,
    down_weight,
):
    ctx_count = lax.axis_size("ctx")
    exp_count = lax.axis_size("exp")
    tokens = stream.shape[1]
    features = stream.shape[2]
    top_count = expert_ids.shape[2]
    expert_total = router_weight.shape[1]
    per_ctx = expert_total // ctx_count
    quarters = exp_count // per_ctx
    capacity = 2 * tokens * top_count // expert_total

    stacked = jnp.stack([gate_weight, up_weight, down_weight], axis=0)
    across = from_partner(stacked, "exp", 2)
    pair = jnp.concatenate([stacked, across], axis=1)
    beside = from_partner(pair, "exp", 1)
    held = jnp.concatenate([pair, beside], axis=1)

    attended = attention(queries, key_rows, value_rows)

    widened = stream[0].astype(jnp.float32)
    mean_square = jnp.mean(widened * widened, axis=-1, keepdims=True)
    normed = (widened * lax.rsqrt(mean_square + 1e-06) * norm_gain.astype(jnp.float32)).astype(
        jnp.bfloat16
    )
    logits = jnp.dot(normed, router_weight, preferred_element_type=jnp.float32)
    chosen = expert_ids[0]
    gate_values = jax.nn.sigmoid(jnp.take_along_axis(logits, chosen, axis=1))
    flat_ids = chosen.reshape(-1)
    onehot = (flat_ids[:, None] == jnp.arange(expert_total, dtype=jnp.int32)[None, :]).astype(
        jnp.int32
    )
    earlier = jnp.cumsum(onehot, axis=0) - onehot
    slot_index = jnp.sum(earlier * onehot, axis=1)
    target = (flat_ids % per_ctx * ctx_count + flat_ids // per_ctx) * capacity + slot_index
    source_rows = jnp.repeat(normed, top_count, axis=0)
    outgoing = (
        jnp.zeros((expert_total * capacity, features), jnp.bfloat16).at[target].set(source_rows)
    )
    outgoing = outgoing.reshape(per_ctx, ctx_count, capacity, features)
    arrived = lax.all_to_all(outgoing, "ctx", split_axis=1, concat_axis=1, tiled=True)
    share = ctx_count // quarters
    to_holders = arrived.reshape(exp_count, share, capacity, features)
    received = lax.all_to_all(to_holders, "exp", split_axis=0, concat_axis=0, tiled=True)
    computed = expert_rows(received.reshape(-1, features), held[0], held[1], held[2])
    computed = computed.astype(jnp.bfloat16).reshape(exp_count, share, capacity, features)
    returned = lax.all_to_all(computed, "exp", split_axis=0, concat_axis=0, tiled=True)
    finished = returned.reshape(per_ctx, ctx_count, capacity, features)
    came_back = lax.all_to_all(finished, "ctx", split_axis=1, concat_axis=1, tiled=True)
    flat_back = came_back.reshape(expert_total * capacity, features)
    picked = (
        jnp.take(flat_back, target, axis=0).astype(jnp.float32).reshape(tokens, top_count, features)
    )
    mixture = jnp.sum(picked * gate_values[:, :, None], axis=1).astype(jnp.bfloat16)
    return (attended, mixture[None])


def solution(mesh):
    placed = (
        P("exp", "ctx", None),
        P("exp", "ctx", None, None),
        P("exp", "ctx", None, None),
        P("exp", "ctx", None, None),
        P("exp", "ctx", None),
        P(),
        P(),
        P(("ctx", "exp"), None),
        P(("ctx", "exp"), None),
        P(("ctx", "exp"), None),
    )
    return jax.shard_map(
        local,
        mesh=mesh,
        in_specs=placed,
        out_specs=(P("exp", "ctx", None, None), P("exp", "ctx", None)),
        check_vma=False,
    )
```

```python
import functools
import math

import jax
import jax.numpy as jnp
from jax import lax
from jax.experimental import pallas as pl
from jax.experimental.pallas import tpu as pltpu
from jax.sharding import PartitionSpec as P


def from_partner(value, axis, flip):
    return lax.ppermute(value, axis, [(i, i ^ flip) for i in range(lax.axis_size(axis))])


def expert_rows(flat_rows, gate_rows, up_rows, down_rows):
    contract = (((1,), (1,)), ((), ()))
    gate_part = lax.dot_general(flat_rows, gate_rows, contract, preferred_element_type=jnp.float32)
    up_part = lax.dot_general(flat_rows, up_rows, contract, preferred_element_type=jnp.float32)
    hidden = (jax.nn.silu(gate_part) * up_part).astype(jnp.bfloat16)
    return jnp.dot(hidden, down_rows, preferred_element_type=jnp.float32)


def _flash_kernel(block, group, scaling, c_ref, qt_ref, k_ref, vt_ref, o_ref, m_sc, l_sc, acc_sc):
    c = c_ref[0]
    qt = qt_ref[0]
    width = qt.shape[1]
    m_sc[...] = jnp.full(m_sc.shape, -1e30, jnp.float32)
    l_sc[...] = jnp.zeros(l_sc.shape, jnp.float32)
    acc_sc[...] = jnp.zeros(acc_sc.shape, jnp.float32)

    def update(j, masked):
        start = pl.multiple_of(j * block, block)
        k = k_ref[0, pl.ds(start, block), :]
        vt = vt_ref[0, :, pl.ds(start, block)]
        s = jnp.dot(k, qt, preferred_element_type=jnp.float32) * scaling
        if masked:
            kpos = lax.broadcasted_iota(jnp.int32, (block, width), 0)
            qpos = lax.broadcasted_iota(jnp.int32, (block, width), 1) // group
            s = jnp.where(kpos <= qpos, s, -1e30)
        m_prev = m_sc[...]
        m_new = jnp.maximum(m_prev, jnp.max(s, axis=0, keepdims=True))
        alpha = jnp.exp(m_prev - m_new)
        p = jnp.exp(s - m_new)
        l_sc[...] = alpha * l_sc[...] + jnp.sum(p, axis=0, keepdims=True)
        acc_sc[...] = alpha * acc_sc[...] + jnp.dot(
            vt, p.astype(jnp.bfloat16), preferred_element_type=jnp.float32
        )
        m_sc[...] = m_new

    def body(j, carry):
        update(j, False)
        return carry

    lax.fori_loop(0, c, body, 0)
    update(c, True)
    o_ref[0] = (acc_sc[...] / l_sc[...]).astype(o_ref.dtype)


def attention(queries, key_rows, value_rows):
    seq_rows = queries.shape[1]
    head_count = queries.shape[2]
    head_size = queries.shape[3]
    kv_count = key_rows.shape[2]
    group_size = head_count // kv_count
    scaling = 1.0 / math.sqrt(head_size)
    width = seq_rows * group_size
    grouped_t = (
        queries[0]
        .reshape(seq_rows, kv_count, group_size, head_size)
        .transpose(1, 3, 0, 2)
        .reshape(kv_count, head_size, width)
    )
    local_kv = jnp.stack([key_rows[0], value_rows[0]], axis=0).transpose(0, 2, 1, 3)
    gathered = lax.all_gather(local_kv, "ctx", axis=2, tiled=True)
    keys_all = gathered[0]
    values_t = gathered[1].transpose(0, 2, 1)
    total_rows = keys_all.shape[1]
    me = lax.axis_index("ctx").astype(jnp.int32).reshape(1)
    out = pl.pallas_call(
        functools.partial(_flash_kernel, seq_rows, group_size, scaling),
        grid_spec=pltpu.PrefetchScalarGridSpec(
            num_scalar_prefetch=1,
            grid=(kv_count,),
            in_specs=[
                pl.BlockSpec((1, head_size, width), lambda g, c: (g, 0, 0)),
                pl.BlockSpec((1, total_rows, head_size), lambda g, c: (g, 0, 0)),
                pl.BlockSpec((1, head_size, total_rows), lambda g, c: (g, 0, 0)),
            ],
            out_specs=pl.BlockSpec((1, head_size, width), lambda g, c: (g, 0, 0)),
            scratch_shapes=[
                pltpu.VMEM((1, width), jnp.float32),
                pltpu.VMEM((1, width), jnp.float32),
                pltpu.VMEM((head_size, width), jnp.float32),
            ],
        ),
        out_shape=jax.ShapeDtypeStruct((kv_count, head_size, width), jnp.bfloat16),
        cost_estimate=pl.CostEstimate(
            flops=2 * kv_count * width * total_rows * head_size,
            transcendentals=kv_count * width * total_rows // 2,
            bytes_accessed=4 * kv_count * total_rows * head_size + 4 * kv_count * width * head_size,
        ),
    )(me, grouped_t, keys_all, values_t)
    return (
        out.reshape(kv_count, head_size, seq_rows, group_size)
        .transpose(2, 0, 3, 1)
        .reshape(1, seq_rows, head_count, head_size)
    )


def local(
    stream,
    queries,
    key_rows,
    value_rows,
    expert_ids,
    norm_gain,
    router_weight,
    gate_weight,
    up_weight,
    down_weight,
):
    ctx_count = lax.axis_size("ctx")
    exp_count = lax.axis_size("exp")
    tokens = stream.shape[1]
    features = stream.shape[2]
    top_count = expert_ids.shape[2]
    expert_total = router_weight.shape[1]
    per_ctx = expert_total // ctx_count
    quarters = exp_count // per_ctx
    capacity = 2 * tokens * top_count // expert_total

    stacked = jnp.stack([gate_weight, up_weight, down_weight], axis=0)
    across = from_partner(stacked, "exp", 2)
    pair = jnp.concatenate([stacked, across], axis=1)
    beside = from_partner(pair, "exp", 1)
    held = jnp.concatenate([pair, beside], axis=1)

    attended = attention(queries, key_rows, value_rows)

    widened = stream[0].astype(jnp.float32)
    mean_square = jnp.mean(widened * widened, axis=-1, keepdims=True)
    normed = (widened * lax.rsqrt(mean_square + 1e-06) * norm_gain.astype(jnp.float32)).astype(
        jnp.bfloat16
    )
    logits = jnp.dot(normed, router_weight, preferred_element_type=jnp.float32)
    chosen = expert_ids[0]
    gate_values = jax.nn.sigmoid(jnp.take_along_axis(logits, chosen, axis=1))
    flat_ids = chosen.reshape(-1)
    onehot = (flat_ids[:, None] == jnp.arange(expert_total, dtype=jnp.int32)[None, :]).astype(
        jnp.int32
    )
    earlier = jnp.cumsum(onehot, axis=0) - onehot
    slot_index = jnp.sum(earlier * onehot, axis=1)
    target = (flat_ids % per_ctx * ctx_count + flat_ids // per_ctx) * capacity + slot_index
    source_rows = jnp.repeat(normed, top_count, axis=0)
    outgoing = (
        jnp.zeros((expert_total * capacity, features), jnp.bfloat16).at[target].set(source_rows)
    )
    outgoing = outgoing.reshape(per_ctx, ctx_count, capacity, features)
    arrived = lax.all_to_all(outgoing, "ctx", split_axis=1, concat_axis=1, tiled=True)
    share = ctx_count // quarters
    to_holders = arrived.reshape(exp_count, share, capacity, features)
    received = lax.all_to_all(to_holders, "exp", split_axis=0, concat_axis=0, tiled=True)
    computed = expert_rows(received.reshape(-1, features), held[0], held[1], held[2])
    computed = computed.astype(jnp.bfloat16).reshape(exp_count, share, capacity, features)
    returned = lax.all_to_all(computed, "exp", split_axis=0, concat_axis=0, tiled=True)
    finished = returned.reshape(per_ctx, ctx_count, capacity, features)
    came_back = lax.all_to_all(finished, "ctx", split_axis=1, concat_axis=1, tiled=True)
    flat_back = came_back.reshape(expert_total * capacity, features)
    picked = (
        jnp.take(flat_back, target, axis=0).astype(jnp.float32).reshape(tokens, top_count, features)
    )
    mixture = jnp.sum(picked * gate_values[:, :, None], axis=1).astype(jnp.bfloat16)
    return (attended, mixture[None])


def solution(mesh):
    placed = (
        P("exp", "ctx", None),
        P("exp", "ctx", None, None),
        P("exp", "ctx", None, None),
        P("exp", "ctx", None, None),
        P("exp", "ctx", None),
        P(),
        P(),
        P(("ctx", "exp"), None),
        P(("ctx", "exp"), None),
        P(("ctx", "exp"), None),
    )
    return jax.shard_map(
        local,
        mesh=mesh,
        in_specs=placed,
        out_specs=(P("exp", "ctx", None, None), P("exp", "ctx", None)),
        check_vma=False,
    )
```

```python
import functools
import math

import jax
import jax.numpy as jnp
from jax import lax
from jax.experimental import pallas as pl
from jax.experimental.pallas import tpu as pltpu
from jax.sharding import PartitionSpec as P


def from_partner(value, axis, flip):
    return lax.ppermute(value, axis, [(i, i ^ flip) for i in range(lax.axis_size(axis))])


def expert_rows(flat_rows, gate_rows, up_rows, down_rows):
    contract = (((1,), (1,)), ((), ()))
    gate_part = lax.dot_general(flat_rows, gate_rows, contract, preferred_element_type=jnp.float32)
    up_part = lax.dot_general(flat_rows, up_rows, contract, preferred_element_type=jnp.float32)
    hidden = (jax.nn.silu(gate_part) * up_part).astype(jnp.bfloat16)
    return jnp.dot(hidden, down_rows, preferred_element_type=jnp.float32)


def _flash_kernel(block, group, scaling, c_ref, qt_ref, k_ref, vt_ref, o_ref, m_sc, l_sc, acc_sc):
    c = c_ref[0]
    qt = qt_ref[0]
    width = qt.shape[1]
    m_sc[...] = jnp.full(m_sc.shape, -1e30, jnp.float32)
    l_sc[...] = jnp.zeros(l_sc.shape, jnp.float32)
    acc_sc[...] = jnp.zeros(acc_sc.shape, jnp.float32)

    def update(j, masked, size=block):
        start = pl.multiple_of(j * size, size)
        k = k_ref[0, pl.ds(start, size), :]
        vt = vt_ref[0, :, pl.ds(start, size)]
        s = jnp.dot(k, qt, preferred_element_type=jnp.float32) * scaling
        if masked:
            kpos = lax.broadcasted_iota(jnp.int32, (block, width), 0)
            qpos = lax.broadcasted_iota(jnp.int32, (block, width), 1) // group
            s = jnp.where(kpos <= qpos, s, -1e30)
        m_prev = m_sc[...]
        m_new = jnp.maximum(m_prev, jnp.max(s, axis=0, keepdims=True))
        alpha = jnp.exp(m_prev - m_new)
        p = jnp.exp(s - m_new)
        l_sc[...] = alpha * l_sc[...] + jnp.sum(p, axis=0, keepdims=True)
        acc_sc[...] = alpha * acc_sc[...] + jnp.dot(
            vt, p.astype(jnp.bfloat16), preferred_element_type=jnp.float32
        )
        m_sc[...] = m_new

    wide = 4 * block
    span = wide // block

    def body_wide(j, carry):
        update(j, False, wide)
        return carry

    def body(j, carry):
        update(j, False)
        return carry

    lax.fori_loop(0, c // span, body_wide, 0)
    lax.fori_loop(c // span * span, c, body, 0)
    update(c, True)
    o_ref[0] = (acc_sc[...] / l_sc[...]).astype(o_ref.dtype)


def attention(queries, key_rows, value_rows):
    seq_rows = queries.shape[1]
    head_count = queries.shape[2]
    head_size = queries.shape[3]
    kv_count = key_rows.shape[2]
    group_size = head_count // kv_count
    scaling = 1.0 / math.sqrt(head_size)
    width = seq_rows * group_size
    grouped_t = (
        queries[0]
        .reshape(seq_rows, kv_count, group_size, head_size)
        .transpose(1, 3, 0, 2)
        .reshape(kv_count, head_size, width)
    )
    local_kv = jnp.stack([key_rows[0], value_rows[0]], axis=0).transpose(0, 2, 1, 3)
    gathered = lax.all_gather(local_kv, "ctx", axis=2, tiled=True)
    keys_all = gathered[0]
    values_t = gathered[1].transpose(0, 2, 1)
    total_rows = keys_all.shape[1]
    me = lax.axis_index("ctx").astype(jnp.int32).reshape(1)
    out = pl.pallas_call(
        functools.partial(_flash_kernel, seq_rows, group_size, scaling),
        grid_spec=pltpu.PrefetchScalarGridSpec(
            num_scalar_prefetch=1,
            grid=(kv_count,),
            in_specs=[
                pl.BlockSpec((1, head_size, width), lambda g, c: (g, 0, 0)),
                pl.BlockSpec((1, total_rows, head_size), lambda g, c: (g, 0, 0)),
                pl.BlockSpec((1, head_size, total_rows), lambda g, c: (g, 0, 0)),
            ],
            out_specs=pl.BlockSpec((1, head_size, width), lambda g, c: (g, 0, 0)),
            scratch_shapes=[
                pltpu.VMEM((1, width), jnp.float32),
                pltpu.VMEM((1, width), jnp.float32),
                pltpu.VMEM((head_size, width), jnp.float32),
            ],
        ),
        out_shape=jax.ShapeDtypeStruct((kv_count, head_size, width), jnp.bfloat16),
        cost_estimate=pl.CostEstimate(
            flops=2 * kv_count * width * total_rows * head_size,
            transcendentals=kv_count * width * total_rows // 2,
            bytes_accessed=4 * kv_count * total_rows * head_size + 4 * kv_count * width * head_size,
        ),
    )(me, grouped_t, keys_all, values_t)
    return (
        out.reshape(kv_count, head_size, seq_rows, group_size)
        .transpose(2, 0, 3, 1)
        .reshape(1, seq_rows, head_count, head_size)
    )


def local(
    stream,
    queries,
    key_rows,
    value_rows,
    expert_ids,
    norm_gain,
    router_weight,
    gate_weight,
    up_weight,
    down_weight,
):
    ctx_count = lax.axis_size("ctx")
    exp_count = lax.axis_size("exp")
    tokens = stream.shape[1]
    features = stream.shape[2]
    top_count = expert_ids.shape[2]
    expert_total = router_weight.shape[1]
    per_ctx = expert_total // ctx_count
    quarters = exp_count // per_ctx
    capacity = 2 * tokens * top_count // expert_total

    stacked = jnp.stack([gate_weight, up_weight, down_weight], axis=0)
    across = from_partner(stacked, "exp", 2)
    pair = jnp.concatenate([stacked, across], axis=1)
    beside = from_partner(pair, "exp", 1)
    held = jnp.concatenate([pair, beside], axis=1)

    attended = attention(queries, key_rows, value_rows)

    widened = stream[0].astype(jnp.float32)
    mean_square = jnp.mean(widened * widened, axis=-1, keepdims=True)
    normed = (widened * lax.rsqrt(mean_square + 1e-06) * norm_gain.astype(jnp.float32)).astype(
        jnp.bfloat16
    )
    logits = jnp.dot(normed, router_weight, preferred_element_type=jnp.float32)
    chosen = expert_ids[0]
    gate_values = jax.nn.sigmoid(jnp.take_along_axis(logits, chosen, axis=1))
    flat_ids = chosen.reshape(-1)
    onehot = (flat_ids[:, None] == jnp.arange(expert_total, dtype=jnp.int32)[None, :]).astype(
        jnp.int32
    )
    earlier = jnp.cumsum(onehot, axis=0) - onehot
    slot_index = jnp.sum(earlier * onehot, axis=1)
    target = (flat_ids % per_ctx * ctx_count + flat_ids // per_ctx) * capacity + slot_index
    source_rows = jnp.repeat(normed, top_count, axis=0)
    outgoing = (
        jnp.zeros((expert_total * capacity, features), jnp.bfloat16).at[target].set(source_rows)
    )
    outgoing = outgoing.reshape(per_ctx, ctx_count, capacity, features)
    arrived = lax.all_to_all(outgoing, "ctx", split_axis=1, concat_axis=1, tiled=True)
    share = ctx_count // quarters
    to_holders = arrived.reshape(exp_count, share, capacity, features)
    received = lax.all_to_all(to_holders, "exp", split_axis=0, concat_axis=0, tiled=True)
    computed = expert_rows(received.reshape(-1, features), held[0], held[1], held[2])
    computed = computed.astype(jnp.bfloat16).reshape(exp_count, share, capacity, features)
    returned = lax.all_to_all(computed, "exp", split_axis=0, concat_axis=0, tiled=True)
    finished = returned.reshape(per_ctx, ctx_count, capacity, features)
    came_back = lax.all_to_all(finished, "ctx", split_axis=1, concat_axis=1, tiled=True)
    attended, came_back = lax.optimization_barrier((attended, came_back))
    flat_back = came_back.reshape(expert_total * capacity, features)
    picked = (
        jnp.take(flat_back, target, axis=0).astype(jnp.float32).reshape(tokens, top_count, features)
    )
    mixture = jnp.sum(picked * gate_values[:, :, None], axis=1).astype(jnp.bfloat16)
    return (attended, mixture[None])


def solution(mesh):
    placed = (
        P("exp", "ctx", None),
        P("exp", "ctx", None, None),
        P("exp", "ctx", None, None),
        P("exp", "ctx", None, None),
        P("exp", "ctx", None),
        P(),
        P(),
        P(("ctx", "exp"), None),
        P(("ctx", "exp"), None),
        P(("ctx", "exp"), None),
    )
    return jax.shard_map(
        local,
        mesh=mesh,
        in_specs=placed,
        out_specs=(P("exp", "ctx", None, None), P("exp", "ctx", None)),
        check_vma=False,
    )
```

```python
import functools
import math

import jax
import jax.numpy as jnp
from jax import lax
from jax.experimental import pallas as pl
from jax.experimental.pallas import tpu as pltpu
from jax.sharding import PartitionSpec as P


def from_partner(value, axis, flip):
    return lax.ppermute(value, axis, [(i, i ^ flip) for i in range(lax.axis_size(axis))])


def expert_rows(flat_rows, gate_rows, up_rows, down_rows):
    contract = (((1,), (1,)), ((), ()))
    gate_part = lax.dot_general(flat_rows, gate_rows, contract, preferred_element_type=jnp.float32)
    up_part = lax.dot_general(flat_rows, up_rows, contract, preferred_element_type=jnp.float32)
    hidden = (jax.nn.silu(gate_part) * up_part).astype(jnp.bfloat16)
    return jnp.dot(hidden, down_rows, preferred_element_type=jnp.float32)


def _flash_kernel(block, group, scaling, c_ref, qt_ref, k_ref, vt_ref, o_ref, m_sc, l_sc, acc_sc):
    c = c_ref[0]
    qt = qt_ref[0]
    width = qt.shape[1]
    m_sc[...] = jnp.full(m_sc.shape, -1e30, jnp.float32)
    l_sc[...] = jnp.zeros(l_sc.shape, jnp.float32)
    acc_sc[...] = jnp.zeros(acc_sc.shape, jnp.float32)

    def update(j, masked, size=block):
        start = pl.multiple_of(j * size, size)
        k = k_ref[0, pl.ds(start, size), :]
        vt = vt_ref[0, :, pl.ds(start, size)]
        s = jnp.dot(k, qt, preferred_element_type=jnp.float32) * scaling
        if masked:
            kpos = lax.broadcasted_iota(jnp.int32, (block, width), 0)
            qpos = lax.broadcasted_iota(jnp.int32, (block, width), 1) // group
            s = jnp.where(kpos <= qpos, s, -1e30)
        m_prev = m_sc[...]
        m_new = jnp.maximum(m_prev, jnp.max(s, axis=0, keepdims=True))
        alpha = jnp.exp(m_prev - m_new)
        p = jnp.exp(s - m_new)
        l_sc[...] = alpha * l_sc[...] + jnp.sum(p, axis=0, keepdims=True)
        acc_sc[...] = alpha * acc_sc[...] + jnp.dot(
            vt, p.astype(jnp.bfloat16), preferred_element_type=jnp.float32
        )
        m_sc[...] = m_new

    wide = 4 * block
    span = wide // block

    def body_wide(j, carry):
        update(j, False, wide)
        return carry

    def body(j, carry):
        update(j, False)
        return carry

    lax.fori_loop(0, c // span, body_wide, 0)
    lax.fori_loop(c // span * span, c, body, 0)
    update(c, True)
    o_ref[0] = (acc_sc[...] / l_sc[...]).astype(o_ref.dtype)


def attention(queries, key_rows, value_rows):
    seq_rows = queries.shape[1]
    head_count = queries.shape[2]
    head_size = queries.shape[3]
    kv_count = key_rows.shape[2]
    group_size = head_count // kv_count
    scaling = 1.0 / math.sqrt(head_size)
    width = seq_rows * group_size
    grouped_t = (
        queries[0]
        .reshape(seq_rows, kv_count, group_size, head_size)
        .transpose(1, 3, 0, 2)
        .reshape(kv_count, head_size, width)
    )
    local_kv = jnp.stack([key_rows[0], value_rows[0]], axis=0).transpose(0, 2, 1, 3)
    gathered = lax.all_gather(local_kv, "ctx", axis=2, tiled=True)
    keys_all = gathered[0]
    values_t = gathered[1].transpose(0, 2, 1)
    total_rows = keys_all.shape[1]
    me = lax.axis_index("ctx").astype(jnp.int32).reshape(1)
    out = pl.pallas_call(
        functools.partial(_flash_kernel, seq_rows, group_size, scaling),
        grid_spec=pltpu.PrefetchScalarGridSpec(
            num_scalar_prefetch=1,
            grid=(kv_count,),
            in_specs=[
                pl.BlockSpec((1, head_size, width), lambda g, c: (g, 0, 0)),
                pl.BlockSpec((1, total_rows, head_size), lambda g, c: (g, 0, 0)),
                pl.BlockSpec((1, head_size, total_rows), lambda g, c: (g, 0, 0)),
            ],
            out_specs=pl.BlockSpec((1, head_size, width), lambda g, c: (g, 0, 0)),
            scratch_shapes=[
                pltpu.VMEM((1, width), jnp.float32),
                pltpu.VMEM((1, width), jnp.float32),
                pltpu.VMEM((head_size, width), jnp.float32),
            ],
        ),
        out_shape=jax.ShapeDtypeStruct((kv_count, head_size, width), jnp.bfloat16),
        cost_estimate=pl.CostEstimate(
            flops=2 * kv_count * width * total_rows * head_size,
            transcendentals=kv_count * width * total_rows // 2,
            bytes_accessed=4 * kv_count * total_rows * head_size + 4 * kv_count * width * head_size,
        ),
    )(me, grouped_t, keys_all, values_t)
    return (
        out.reshape(kv_count, head_size, seq_rows, group_size)
        .transpose(2, 0, 3, 1)
        .reshape(1, seq_rows, head_count, head_size)
    )


def local(
    stream,
    queries,
    key_rows,
    value_rows,
    expert_ids,
    norm_gain,
    router_weight,
    gate_weight,
    up_weight,
    down_weight,
):
    ctx_count = lax.axis_size("ctx")
    exp_count = lax.axis_size("exp")
    tokens = stream.shape[1]
    features = stream.shape[2]
    top_count = expert_ids.shape[2]
    expert_total = router_weight.shape[1]
    per_ctx = expert_total // ctx_count
    quarters = exp_count // per_ctx
    capacity = 2 * tokens * top_count // expert_total

    stacked = jnp.stack([gate_weight, up_weight, down_weight], axis=0)
    across = from_partner(stacked, "exp", 2)
    pair = jnp.concatenate([stacked, across], axis=1)
    beside = from_partner(pair, "exp", 1)
    held = jnp.concatenate([pair, beside], axis=1)

    attended = attention(queries, key_rows, value_rows)

    widened = stream[0].astype(jnp.float32)
    mean_square = jnp.mean(widened * widened, axis=-1, keepdims=True)
    normed = (widened * lax.rsqrt(mean_square + 1e-06) * norm_gain.astype(jnp.float32)).astype(
        jnp.bfloat16
    )
    logits = jnp.dot(normed, router_weight, preferred_element_type=jnp.float32)
    chosen = expert_ids[0]
    gate_values = jax.nn.sigmoid(jnp.take_along_axis(logits, chosen, axis=1))
    flat_ids = chosen.reshape(-1)
    onehot = (flat_ids[:, None] == jnp.arange(expert_total, dtype=jnp.int32)[None, :]).astype(
        jnp.int32
    )
    earlier = jnp.cumsum(onehot, axis=0) - onehot
    slot_index = jnp.sum(earlier * onehot, axis=1)
    target = flat_ids * capacity + slot_index
    source_rows = jnp.repeat(normed, top_count, axis=0)
    outgoing = (
        jnp.zeros((expert_total * capacity, features), jnp.bfloat16).at[target].set(source_rows)
    )
    grid_axes = ("ctx", "exp")
    received = lax.all_to_all(outgoing, grid_axes, split_axis=0, concat_axis=0, tiled=True)
    computed = expert_rows(received, held[0], held[1], held[2]).astype(jnp.bfloat16)
    came_back = lax.all_to_all(computed, grid_axes, split_axis=0, concat_axis=0, tiled=True)
    attended, came_back = lax.optimization_barrier((attended, came_back))
    flat_back = came_back.reshape(expert_total * capacity, features)
    picked = (
        jnp.take(flat_back, target, axis=0).astype(jnp.float32).reshape(tokens, top_count, features)
    )
    mixture = jnp.sum(picked * gate_values[:, :, None], axis=1).astype(jnp.bfloat16)
    return (attended, mixture[None])


def solution(mesh):
    placed = (
        P("exp", "ctx", None),
        P("exp", "ctx", None, None),
        P("exp", "ctx", None, None),
        P("exp", "ctx", None, None),
        P("exp", "ctx", None),
        P(),
        P(),
        P(("ctx", "exp"), None),
        P(("ctx", "exp"), None),
        P(("ctx", "exp"), None),
    )
    return jax.shard_map(
        local,
        mesh=mesh,
        in_specs=placed,
        out_specs=(P("exp", "ctx", None, None), P("exp", "ctx", None)),
        check_vma=False,
    )
```

```python
import functools
import math

import jax
import jax.numpy as jnp
from jax import lax
from jax.experimental import pallas as pl
from jax.experimental.pallas import tpu as pltpu
from jax.sharding import PartitionSpec as P


def from_partner(value, axis, flip):
    return lax.ppermute(value, axis, [(i, i ^ flip) for i in range(lax.axis_size(axis))])


def expert_rows(flat_rows, gate_rows, up_rows, down_rows):
    contract = (((1,), (1,)), ((), ()))
    gate_part = lax.dot_general(flat_rows, gate_rows, contract, preferred_element_type=jnp.float32)
    up_part = lax.dot_general(flat_rows, up_rows, contract, preferred_element_type=jnp.float32)
    hidden = (jax.nn.silu(gate_part) * up_part).astype(jnp.bfloat16)
    return jnp.dot(hidden, down_rows, preferred_element_type=jnp.float32)


def _flash_kernel(block, group, scaling, c_ref, qt_ref, k_ref, vt_ref, o_ref, m_sc, l_sc, acc_sc):
    c = c_ref[0]
    qt = qt_ref[0]
    width = qt.shape[1]
    m_sc[...] = jnp.full(m_sc.shape, -1e30, jnp.float32)
    l_sc[...] = jnp.zeros(l_sc.shape, jnp.float32)
    acc_sc[...] = jnp.zeros(acc_sc.shape, jnp.float32)

    def update(j, masked, size=block):
        start = pl.multiple_of(j * size, size)
        k = k_ref[0, pl.ds(start, size), :]
        vt = vt_ref[0, :, pl.ds(start, size)]
        s = jnp.dot(k, qt, preferred_element_type=jnp.float32) * scaling
        if masked:
            kpos = lax.broadcasted_iota(jnp.int32, (block, width), 0)
            qpos = lax.broadcasted_iota(jnp.int32, (block, width), 1) // group
            s = jnp.where(kpos <= qpos, s, -1e30)
        m_prev = m_sc[...]
        m_new = jnp.maximum(m_prev, jnp.max(s, axis=0, keepdims=True))
        alpha = jnp.exp(m_prev - m_new)
        p = jnp.exp(s - m_new)
        l_sc[...] = alpha * l_sc[...] + jnp.sum(p, axis=0, keepdims=True)
        acc_sc[...] = alpha * acc_sc[...] + jnp.dot(
            vt, p.astype(jnp.bfloat16), preferred_element_type=jnp.float32
        )
        m_sc[...] = m_new

    wide = 4 * block
    span = wide // block

    def body_wide(j, carry):
        update(j, False, wide)
        return carry

    def body(j, carry):
        update(j, False)
        return carry

    lax.fori_loop(0, c // span, body_wide, 0)
    lax.fori_loop(c // span * span, c, body, 0)
    update(c, True)
    o_ref[0] = (acc_sc[...] / l_sc[...]).astype(o_ref.dtype)


def gather_attention_inputs(queries, key_rows, value_rows):
    local_kv = jnp.stack([key_rows[0], value_rows[0]], axis=0).transpose(0, 2, 1, 3)
    gathered = lax.all_gather(local_kv, "ctx", axis=2, tiled=True)
    return queries, gathered


def attention(queries, gathered):
    seq_rows = queries.shape[1]
    head_count = queries.shape[2]
    head_size = queries.shape[3]
    kv_count = gathered.shape[1]
    group_size = head_count // kv_count
    scaling = 1.0 / math.sqrt(head_size)
    width = seq_rows * group_size
    grouped_t = (
        queries[0]
        .reshape(seq_rows, kv_count, group_size, head_size)
        .transpose(1, 3, 0, 2)
        .reshape(kv_count, head_size, width)
    )
    keys_all = gathered[0]
    values_t = gathered[1].transpose(0, 2, 1)
    total_rows = keys_all.shape[1]
    me = lax.axis_index("ctx").astype(jnp.int32).reshape(1)
    out = pl.pallas_call(
        functools.partial(_flash_kernel, seq_rows, group_size, scaling),
        grid_spec=pltpu.PrefetchScalarGridSpec(
            num_scalar_prefetch=1,
            grid=(kv_count,),
            in_specs=[
                pl.BlockSpec((1, head_size, width), lambda g, c: (g, 0, 0)),
                pl.BlockSpec((1, total_rows, head_size), lambda g, c: (g, 0, 0)),
                pl.BlockSpec((1, head_size, total_rows), lambda g, c: (g, 0, 0)),
            ],
            out_specs=pl.BlockSpec((1, head_size, width), lambda g, c: (g, 0, 0)),
            scratch_shapes=[
                pltpu.VMEM((1, width), jnp.float32),
                pltpu.VMEM((1, width), jnp.float32),
                pltpu.VMEM((head_size, width), jnp.float32),
            ],
        ),
        out_shape=jax.ShapeDtypeStruct((kv_count, head_size, width), jnp.bfloat16),
        cost_estimate=pl.CostEstimate(
            flops=2 * kv_count * width * total_rows * head_size,
            transcendentals=kv_count * width * total_rows // 2,
            bytes_accessed=4 * kv_count * total_rows * head_size + 4 * kv_count * width * head_size,
        ),
    )(me, grouped_t, keys_all, values_t)
    return (
        out.reshape(kv_count, head_size, seq_rows, group_size)
        .transpose(2, 0, 3, 1)
        .reshape(1, seq_rows, head_count, head_size)
    )


def local(
    stream,
    queries,
    key_rows,
    value_rows,
    expert_ids,
    norm_gain,
    router_weight,
    gate_weight,
    up_weight,
    down_weight,
):
    ctx_count = lax.axis_size("ctx")
    exp_count = lax.axis_size("exp")
    tokens = stream.shape[1]
    features = stream.shape[2]
    top_count = expert_ids.shape[2]
    expert_total = router_weight.shape[1]
    per_ctx = expert_total // ctx_count
    quarters = exp_count // per_ctx
    capacity = 2 * tokens * top_count // expert_total

    attention_inputs = gather_attention_inputs(queries, key_rows, value_rows)
    stacked = jnp.stack([gate_weight, up_weight, down_weight], axis=0)
    across = from_partner(stacked, "exp", 2)

    widened = stream[0].astype(jnp.float32)
    mean_square = jnp.mean(widened * widened, axis=-1, keepdims=True)
    normed = (widened * lax.rsqrt(mean_square + 1e-06) * norm_gain.astype(jnp.float32)).astype(
        jnp.bfloat16
    )
    logits = jnp.dot(normed, router_weight, preferred_element_type=jnp.float32)
    chosen = expert_ids[0]
    gate_values = jax.nn.sigmoid(jnp.take_along_axis(logits, chosen, axis=1))
    flat_ids = chosen.reshape(-1)
    onehot = (flat_ids[:, None] == jnp.arange(expert_total, dtype=jnp.int32)[None, :]).astype(
        jnp.int32
    )
    earlier = jnp.cumsum(onehot, axis=0) - onehot
    slot_index = jnp.sum(earlier * onehot, axis=1)
    target = flat_ids * capacity + slot_index
    source_rows = jnp.repeat(normed, top_count, axis=0)
    outgoing = (
        jnp.zeros((expert_total * capacity, features), jnp.bfloat16).at[target].set(source_rows)
    )
    across, outgoing = lax.optimization_barrier((across, outgoing))
    pair = jnp.concatenate([stacked, across], axis=1)
    beside = from_partner(pair, "exp", 1)
    held = jnp.concatenate([pair, beside], axis=1)
    grid_axes = ("ctx", "exp")
    received = lax.all_to_all(outgoing, grid_axes, split_axis=0, concat_axis=0, tiled=True)
    computed = expert_rows(received, held[0], held[1], held[2]).astype(jnp.bfloat16)
    attention_inputs, computed = lax.optimization_barrier((attention_inputs, computed))
    attended = attention(*attention_inputs)
    came_back = lax.all_to_all(computed, grid_axes, split_axis=0, concat_axis=0, tiled=True)
    attended, came_back = lax.optimization_barrier((attended, came_back))
    flat_back = came_back.reshape(expert_total * capacity, features)
    picked = (
        jnp.take(flat_back, target, axis=0).astype(jnp.float32).reshape(tokens, top_count, features)
    )
    mixture = jnp.sum(picked * gate_values[:, :, None], axis=1).astype(jnp.bfloat16)
    return (attended, mixture[None])


def solution(mesh):
    placed = (
        P("exp", "ctx", None),
        P("exp", "ctx", None, None),
        P("exp", "ctx", None, None),
        P("exp", "ctx", None, None),
        P("exp", "ctx", None),
        P(),
        P(),
        P(("ctx", "exp"), None),
        P(("ctx", "exp"), None),
        P(("ctx", "exp"), None),
    )
    return jax.shard_map(
        local,
        mesh=mesh,
        in_specs=placed,
        out_specs=(P("exp", "ctx", None, None), P("exp", "ctx", None)),
        check_vma=False,
    )
```

```python
import functools
import math

import jax
import jax.numpy as jnp
from jax import lax
from jax.experimental import pallas as pl
from jax.experimental.pallas import tpu as pltpu
from jax.sharding import PartitionSpec as P


def from_partner(value, axis, flip):
    return lax.ppermute(value, axis, [(i, i ^ flip) for i in range(lax.axis_size(axis))])


def expert_rows(flat_rows, gate_rows, up_rows, down_rows):
    contract = (((1,), (1,)), ((), ()))
    gate_part = lax.dot_general(flat_rows, gate_rows, contract, preferred_element_type=jnp.float32)
    up_part = lax.dot_general(flat_rows, up_rows, contract, preferred_element_type=jnp.float32)
    hidden = (jax.nn.silu(gate_part) * up_part).astype(jnp.bfloat16)
    return jnp.dot(hidden, down_rows, preferred_element_type=jnp.float32)


def _flash_kernel(block, group, scaling, c_ref, qt_ref, k_ref, vt_ref, o_ref, m_sc, l_sc, acc_sc):
    c = c_ref[0]
    qt = qt_ref[0]
    width = qt.shape[1]
    m_sc[...] = jnp.full(m_sc.shape, -1e30, jnp.float32)
    l_sc[...] = jnp.zeros(l_sc.shape, jnp.float32)
    acc_sc[...] = jnp.zeros(acc_sc.shape, jnp.float32)

    def update(j, masked, size=block):
        start = pl.multiple_of(j * size, size)
        k = k_ref[0, pl.ds(start, size), :]
        vt = vt_ref[0, :, pl.ds(start, size)]
        s = jnp.dot(k, qt, preferred_element_type=jnp.float32) * scaling
        if masked:
            kpos = lax.broadcasted_iota(jnp.int32, (block, width), 0)
            qpos = lax.broadcasted_iota(jnp.int32, (block, width), 1) // group
            s = jnp.where(kpos <= qpos, s, -1e30)
        m_prev = m_sc[...]
        m_new = jnp.maximum(m_prev, jnp.max(s, axis=0, keepdims=True))
        alpha = jnp.exp(m_prev - m_new)
        p = jnp.exp(s - m_new)
        l_sc[...] = alpha * l_sc[...] + jnp.sum(p, axis=0, keepdims=True)
        acc_sc[...] = alpha * acc_sc[...] + jnp.dot(
            vt, p.astype(jnp.bfloat16), preferred_element_type=jnp.float32
        )
        m_sc[...] = m_new

    wide = 4 * block
    span = wide // block

    def body_wide(j, carry):
        update(j, False, wide)
        return carry

    def body(j, carry):
        update(j, False)
        return carry

    lax.fori_loop(0, c // span, body_wide, 0)
    lax.fori_loop(c // span * span, c, body, 0)
    update(c, True)
    o_ref[0] = (acc_sc[...] / l_sc[...]).astype(o_ref.dtype)


def gather_attention_inputs(queries, key_rows, value_rows):
    local_kv = jnp.stack([key_rows[0], value_rows[0]], axis=0).transpose(0, 2, 1, 3)
    gathered = lax.all_gather(local_kv, "ctx", axis=2, tiled=True)
    return queries, gathered


def attention(queries, gathered):
    seq_rows = queries.shape[1]
    head_count = queries.shape[2]
    head_size = queries.shape[3]
    kv_count = gathered.shape[1]
    group_size = head_count // kv_count
    scaling = 1.0 / math.sqrt(head_size)
    width = seq_rows * group_size
    grouped_t = (
        queries[0]
        .reshape(seq_rows, kv_count, group_size, head_size)
        .transpose(1, 3, 0, 2)
        .reshape(kv_count, head_size, width)
    )
    keys_all = gathered[0]
    values_t = gathered[1].transpose(0, 2, 1)
    total_rows = keys_all.shape[1]
    me = lax.axis_index("ctx").astype(jnp.int32).reshape(1)
    out = pl.pallas_call(
        functools.partial(_flash_kernel, seq_rows, group_size, scaling),
        grid_spec=pltpu.PrefetchScalarGridSpec(
            num_scalar_prefetch=1,
            grid=(kv_count,),
            in_specs=[
                pl.BlockSpec((1, head_size, width), lambda g, c: (g, 0, 0)),
                pl.BlockSpec((1, total_rows, head_size), lambda g, c: (g, 0, 0)),
                pl.BlockSpec((1, head_size, total_rows), lambda g, c: (g, 0, 0)),
            ],
            out_specs=pl.BlockSpec((1, head_size, width), lambda g, c: (g, 0, 0)),
            scratch_shapes=[
                pltpu.VMEM((1, width), jnp.float32),
                pltpu.VMEM((1, width), jnp.float32),
                pltpu.VMEM((head_size, width), jnp.float32),
            ],
        ),
        out_shape=jax.ShapeDtypeStruct((kv_count, head_size, width), jnp.bfloat16),
        cost_estimate=pl.CostEstimate(
            flops=2 * kv_count * width * total_rows * head_size,
            transcendentals=kv_count * width * total_rows // 2,
            bytes_accessed=4 * kv_count * total_rows * head_size + 4 * kv_count * width * head_size,
        ),
    )(me, grouped_t, keys_all, values_t)
    return (
        out.reshape(kv_count, head_size, seq_rows, group_size)
        .transpose(2, 0, 3, 1)
        .reshape(1, seq_rows, head_count, head_size)
    )


def local(
    stream,
    queries,
    key_rows,
    value_rows,
    expert_ids,
    norm_gain,
    router_weight,
    gate_weight,
    up_weight,
    down_weight,
):
    ctx_count = lax.axis_size("ctx")
    exp_count = lax.axis_size("exp")
    tokens = stream.shape[1]
    features = stream.shape[2]
    top_count = expert_ids.shape[2]
    expert_total = router_weight.shape[1]
    per_ctx = expert_total // ctx_count
    quarters = exp_count // per_ctx
    capacity = 2 * tokens * top_count // expert_total

    attention_inputs = gather_attention_inputs(queries, key_rows, value_rows)
    stacked = jnp.stack([gate_weight, up_weight, down_weight], axis=0)
    across = from_partner(stacked, "exp", 2)
    own_beside = from_partner(stacked, "exp", 1)

    widened = stream[0].astype(jnp.float32)
    mean_square = jnp.mean(widened * widened, axis=-1, keepdims=True)
    normed = (widened * lax.rsqrt(mean_square + 1e-06) * norm_gain.astype(jnp.float32)).astype(
        jnp.bfloat16
    )
    logits = jnp.dot(normed, router_weight, preferred_element_type=jnp.float32)
    chosen = expert_ids[0]
    gate_values = jax.nn.sigmoid(jnp.take_along_axis(logits, chosen, axis=1))
    flat_ids = chosen.reshape(-1)
    onehot = (flat_ids[:, None] == jnp.arange(expert_total, dtype=jnp.int32)[None, :]).astype(
        jnp.int32
    )
    earlier = jnp.cumsum(onehot, axis=0) - onehot
    slot_index = jnp.sum(earlier * onehot, axis=1)
    target = flat_ids * capacity + slot_index
    tile_rows = 8
    tile = (tile_rows, features // tile_rows)
    source_rows = jnp.repeat(normed, top_count, axis=0).reshape(-1, *tile)
    outgoing = jnp.zeros((expert_total * capacity, *tile), jnp.bfloat16).at[target].set(source_rows)
    grid_axes = ("ctx", "exp")
    received = lax.all_to_all(outgoing, grid_axes, split_axis=0, concat_axis=0, tiled=True)
    across, received = lax.optimization_barrier((across, received))
    across_beside = from_partner(across, "exp", 1)
    held = jnp.concatenate([stacked, across, own_beside, across_beside], axis=1)
    received = received.reshape(-1, features)
    computed = expert_rows(received, held[0], held[1], held[2]).astype(jnp.bfloat16)
    computed = computed.reshape(-1, *tile)
    attention_inputs, computed = lax.optimization_barrier((attention_inputs, computed))
    attended = attention(*attention_inputs)
    came_back = lax.all_to_all(computed, grid_axes, split_axis=0, concat_axis=0, tiled=True)
    attended, came_back = lax.optimization_barrier((attended, came_back))
    flat_back = came_back.reshape(expert_total * capacity, features)
    picked = (
        jnp.take(flat_back, target, axis=0).astype(jnp.float32).reshape(tokens, top_count, features)
    )
    mixture = jnp.sum(picked * gate_values[:, :, None], axis=1).astype(jnp.bfloat16)
    return (attended, mixture[None])


def solution(mesh):
    placed = (
        P("exp", "ctx", None),
        P("exp", "ctx", None, None),
        P("exp", "ctx", None, None),
        P("exp", "ctx", None, None),
        P("exp", "ctx", None),
        P(),
        P(),
        P(("ctx", "exp"), None),
        P(("ctx", "exp"), None),
        P(("ctx", "exp"), None),
    )
    return jax.shard_map(
        local,
        mesh=mesh,
        in_specs=placed,
        out_specs=(P("exp", "ctx", None, None), P("exp", "ctx", None)),
        check_vma=False,
    )
```

```python
import functools
import math

import jax
import jax.numpy as jnp
from jax import lax
from jax.experimental import pallas as pl
from jax.experimental.pallas import tpu as pltpu
from jax.sharding import PartitionSpec as P


def from_partner(value, axis, flip):
    return lax.ppermute(value, axis, [(i, i ^ flip) for i in range(lax.axis_size(axis))])


def expert_rows(flat_rows, gate_rows, up_rows, down_rows):
    contract = (((1,), (1,)), ((), ()))
    gate_part = lax.dot_general(flat_rows, gate_rows, contract, preferred_element_type=jnp.float32)
    up_part = lax.dot_general(flat_rows, up_rows, contract, preferred_element_type=jnp.float32)
    hidden = (jax.nn.silu(gate_part) * up_part).astype(jnp.bfloat16)
    return jnp.dot(hidden, down_rows, preferred_element_type=jnp.float32)


def _flash_kernel(block, group, scaling, c_ref, qt_ref, k_ref, vt_ref, o_ref, m_sc, l_sc, acc_sc):
    c = c_ref[0]
    qt = qt_ref[0]
    width = qt.shape[1]
    m_sc[...] = jnp.full(m_sc.shape, -1e30, jnp.float32)
    l_sc[...] = jnp.zeros(l_sc.shape, jnp.float32)
    acc_sc[...] = jnp.zeros(acc_sc.shape, jnp.float32)

    def update(j, masked, size=block):
        start = pl.multiple_of(j * size, size)
        k = k_ref[0, pl.ds(start, size), :]
        vt = vt_ref[0, :, pl.ds(start, size)]
        s = jnp.dot(k, qt, preferred_element_type=jnp.float32) * scaling
        if masked:
            kpos = lax.broadcasted_iota(jnp.int32, (block, width), 0)
            qpos = lax.broadcasted_iota(jnp.int32, (block, width), 1) // group
            s = jnp.where(kpos <= qpos, s, -1e30)
        m_prev = m_sc[...]
        m_new = jnp.maximum(m_prev, jnp.max(s, axis=0, keepdims=True))
        alpha = jnp.exp(m_prev - m_new)
        p = jnp.exp(s - m_new)
        l_sc[...] = alpha * l_sc[...] + jnp.sum(p, axis=0, keepdims=True)
        acc_sc[...] = alpha * acc_sc[...] + jnp.dot(
            vt, p.astype(jnp.bfloat16), preferred_element_type=jnp.float32
        )
        m_sc[...] = m_new

    wide = 4 * block
    span = wide // block

    def body_wide(j, carry):
        update(j, False, wide)
        return carry

    def body(j, carry):
        update(j, False)
        return carry

    lax.fori_loop(0, c // span, body_wide, 0)
    lax.fori_loop(c // span * span, c, body, 0)
    update(c, True)
    o_ref[0] = (acc_sc[...] / l_sc[...]).astype(o_ref.dtype)


def gather_attention_inputs(queries, key_rows, value_rows):
    local_kv = jnp.stack([key_rows[0], value_rows[0]], axis=0).transpose(0, 2, 1, 3)
    gathered = lax.all_gather(local_kv, "ctx", axis=2, tiled=True)
    return queries, gathered


def attention(queries, gathered):
    seq_rows = queries.shape[1]
    head_count = queries.shape[2]
    head_size = queries.shape[3]
    kv_count = gathered.shape[1]
    group_size = head_count // kv_count
    scaling = 1.0 / math.sqrt(head_size)
    width = seq_rows * group_size
    grouped_t = (
        queries[0]
        .reshape(seq_rows, kv_count, group_size, head_size)
        .transpose(1, 3, 0, 2)
        .reshape(kv_count, head_size, width)
    )
    keys_all = gathered[0]
    values_t = gathered[1].transpose(0, 2, 1)
    total_rows = keys_all.shape[1]
    me = lax.axis_index("ctx").astype(jnp.int32).reshape(1)
    out = pl.pallas_call(
        functools.partial(_flash_kernel, seq_rows, group_size, scaling),
        grid_spec=pltpu.PrefetchScalarGridSpec(
            num_scalar_prefetch=1,
            grid=(kv_count,),
            in_specs=[
                pl.BlockSpec((1, head_size, width), lambda g, c: (g, 0, 0)),
                pl.BlockSpec((1, total_rows, head_size), lambda g, c: (g, 0, 0)),
                pl.BlockSpec((1, head_size, total_rows), lambda g, c: (g, 0, 0)),
            ],
            out_specs=pl.BlockSpec((1, head_size, width), lambda g, c: (g, 0, 0)),
            scratch_shapes=[
                pltpu.VMEM((1, width), jnp.float32),
                pltpu.VMEM((1, width), jnp.float32),
                pltpu.VMEM((head_size, width), jnp.float32),
            ],
        ),
        out_shape=jax.ShapeDtypeStruct((kv_count, head_size, width), jnp.bfloat16),
        cost_estimate=pl.CostEstimate(
            flops=2 * kv_count * width * total_rows * head_size,
            transcendentals=kv_count * width * total_rows // 2,
            bytes_accessed=4 * kv_count * total_rows * head_size + 4 * kv_count * width * head_size,
        ),
    )(me, grouped_t, keys_all, values_t)
    return (
        out.reshape(kv_count, head_size, seq_rows, group_size)
        .transpose(2, 0, 3, 1)
        .reshape(1, seq_rows, head_count, head_size)
    )


def local(
    stream,
    queries,
    key_rows,
    value_rows,
    expert_ids,
    norm_gain,
    router_weight,
    gate_weight,
    up_weight,
    down_weight,
):
    ctx_count = lax.axis_size("ctx")
    exp_count = lax.axis_size("exp")
    tokens = stream.shape[1]
    features = stream.shape[2]
    top_count = expert_ids.shape[2]
    expert_total = router_weight.shape[1]
    per_ctx = expert_total // ctx_count
    quarters = exp_count // per_ctx
    capacity = 2 * tokens * top_count // expert_total

    attention_inputs = gather_attention_inputs(queries, key_rows, value_rows)
    stacked = jnp.stack([gate_weight, up_weight, down_weight], axis=0)
    across = from_partner(stacked, "exp", 2)
    own_beside = from_partner(stacked, "exp", 1)

    widened = stream[0].astype(jnp.float32)
    mean_square = jnp.mean(widened * widened, axis=-1, keepdims=True)
    normed = (widened * lax.rsqrt(mean_square + 1e-06) * norm_gain.astype(jnp.float32)).astype(
        jnp.bfloat16
    )
    logits = jnp.dot(normed, router_weight, preferred_element_type=jnp.float32)
    chosen = expert_ids[0]
    gate_values = jax.nn.sigmoid(jnp.take_along_axis(logits, chosen, axis=1))
    flat_ids = chosen.reshape(-1)
    onehot = (flat_ids[:, None] == jnp.arange(expert_total, dtype=jnp.int32)[None, :]).astype(
        jnp.int32
    )
    earlier = jnp.cumsum(onehot, axis=0) - onehot
    slot_index = jnp.sum(earlier * onehot, axis=1)
    target = flat_ids * capacity + slot_index
    tile_rows = 8
    tile = (tile_rows, features // tile_rows)
    source_rows = jnp.repeat(normed, top_count, axis=0)
    outgoing = (
        jnp.zeros((expert_total * capacity, features), jnp.bfloat16).at[target].set(source_rows)
    )
    outgoing = outgoing.reshape(-1, *tile)
    grid_axes = ("ctx", "exp")
    received = lax.all_to_all(outgoing, grid_axes, split_axis=0, concat_axis=0, tiled=True)
    across, received = lax.optimization_barrier((across, received))
    across_beside = from_partner(across, "exp", 1)
    held = jnp.concatenate([stacked, across, own_beside, across_beside], axis=1)
    received = received.reshape(-1, features)
    computed = expert_rows(received, held[0], held[1], held[2]).astype(jnp.bfloat16)
    computed = computed.reshape(-1, *tile)
    attention_inputs, computed = lax.optimization_barrier((attention_inputs, computed))
    attended = attention(*attention_inputs)
    came_back = lax.all_to_all(computed, grid_axes, split_axis=0, concat_axis=0, tiled=True)
    attended, came_back = lax.optimization_barrier((attended, came_back))
    flat_back = came_back.reshape(expert_total * capacity, features)
    picked = (
        jnp.take(flat_back, target, axis=0).astype(jnp.float32).reshape(tokens, top_count, features)
    )
    mixture = jnp.sum(picked * gate_values[:, :, None], axis=1).astype(jnp.bfloat16)
    return (attended, mixture[None])


def solution(mesh):
    placed = (
        P("exp", "ctx", None),
        P("exp", "ctx", None, None),
        P("exp", "ctx", None, None),
        P("exp", "ctx", None, None),
        P("exp", "ctx", None),
        P(),
        P(),
        P(("ctx", "exp"), None),
        P(("ctx", "exp"), None),
        P(("ctx", "exp"), None),
    )
    return jax.shard_map(
        local,
        mesh=mesh,
        in_specs=placed,
        out_specs=(P("exp", "ctx", None, None), P("exp", "ctx", None)),
        check_vma=False,
    )
```

```python
import functools
import math

import jax
import jax.numpy as jnp
from jax import lax
from jax.experimental import pallas as pl
from jax.experimental.pallas import tpu as pltpu
from jax.sharding import PartitionSpec as P


def from_partner(value, axis, flip):
    return lax.ppermute(value, axis, [(i, i ^ flip) for i in range(lax.axis_size(axis))])


def expert_rows(flat_rows, gate_rows, up_rows, down_rows):
    contract = (((1,), (1,)), ((), ()))
    gate_part = lax.dot_general(flat_rows, gate_rows, contract, preferred_element_type=jnp.float32)
    up_part = lax.dot_general(flat_rows, up_rows, contract, preferred_element_type=jnp.float32)
    hidden = (jax.nn.silu(gate_part) * up_part).astype(jnp.bfloat16)
    return jnp.dot(hidden, down_rows, preferred_element_type=jnp.float32)


def _flash_kernel(block, group, scaling, c_ref, qt_ref, k_ref, vt_ref, o_ref, m_sc, l_sc, acc_sc):
    c = c_ref[0]
    qt = qt_ref[0]
    width = qt.shape[1]
    m_sc[...] = jnp.full(m_sc.shape, -1e30, jnp.float32)
    l_sc[...] = jnp.zeros(l_sc.shape, jnp.float32)
    acc_sc[...] = jnp.zeros(acc_sc.shape, jnp.float32)

    def update(j, masked, size=block):
        start = pl.multiple_of(j * size, size)
        k = k_ref[0, pl.ds(start, size), :]
        vt = vt_ref[0, :, pl.ds(start, size)]
        s = jnp.dot(k, qt, preferred_element_type=jnp.float32) * scaling
        if masked:
            kpos = lax.broadcasted_iota(jnp.int32, (block, width), 0)
            qpos = lax.broadcasted_iota(jnp.int32, (block, width), 1) // group
            s = jnp.where(kpos <= qpos, s, -1e30)
        m_prev = m_sc[...]
        m_new = jnp.maximum(m_prev, jnp.max(s, axis=0, keepdims=True))
        alpha = jnp.exp(m_prev - m_new)
        p = jnp.exp(s - m_new)
        l_sc[...] = alpha * l_sc[...] + jnp.sum(p, axis=0, keepdims=True)
        acc_sc[...] = alpha * acc_sc[...] + jnp.dot(
            vt, p.astype(jnp.bfloat16), preferred_element_type=jnp.float32
        )
        m_sc[...] = m_new

    wide = 4 * block
    span = wide // block

    def body_wide(j, carry):
        update(j, False, wide)
        return carry

    def body(j, carry):
        update(j, False)
        return carry

    lax.fori_loop(0, c // span, body_wide, 0)
    lax.fori_loop(c // span * span, c, body, 0)
    update(c, True)
    o_ref[0] = (acc_sc[...] / l_sc[...]).astype(o_ref.dtype)


def gather_attention_inputs(queries, key_rows, value_rows):
    local_kv = jnp.stack([key_rows[0], value_rows[0]], axis=0).transpose(0, 2, 1, 3)
    gathered = lax.all_gather(local_kv, "ctx", axis=2, tiled=True)
    return queries, gathered


def attention(queries, gathered):
    seq_rows = queries.shape[1]
    head_count = queries.shape[2]
    head_size = queries.shape[3]
    kv_count = gathered.shape[1]
    group_size = head_count // kv_count
    scaling = 1.0 / math.sqrt(head_size)
    width = seq_rows * group_size
    grouped_t = (
        queries[0]
        .reshape(seq_rows, kv_count, group_size, head_size)
        .transpose(1, 3, 0, 2)
        .reshape(kv_count, head_size, width)
    )
    keys_all = gathered[0]
    values_t = gathered[1].transpose(0, 2, 1)
    total_rows = keys_all.shape[1]
    me = lax.axis_index("ctx").astype(jnp.int32).reshape(1)
    out = pl.pallas_call(
        functools.partial(_flash_kernel, seq_rows, group_size, scaling),
        grid_spec=pltpu.PrefetchScalarGridSpec(
            num_scalar_prefetch=1,
            grid=(kv_count,),
            in_specs=[
                pl.BlockSpec((1, head_size, width), lambda g, c: (g, 0, 0)),
                pl.BlockSpec((1, total_rows, head_size), lambda g, c: (g, 0, 0)),
                pl.BlockSpec((1, head_size, total_rows), lambda g, c: (g, 0, 0)),
            ],
            out_specs=pl.BlockSpec((1, head_size, width), lambda g, c: (g, 0, 0)),
            scratch_shapes=[
                pltpu.VMEM((1, width), jnp.float32),
                pltpu.VMEM((1, width), jnp.float32),
                pltpu.VMEM((head_size, width), jnp.float32),
            ],
        ),
        out_shape=jax.ShapeDtypeStruct((kv_count, head_size, width), jnp.bfloat16),
        cost_estimate=pl.CostEstimate(
            flops=2 * kv_count * width * total_rows * head_size,
            transcendentals=kv_count * width * total_rows // 2,
            bytes_accessed=4 * kv_count * total_rows * head_size + 4 * kv_count * width * head_size,
        ),
    )(me, grouped_t, keys_all, values_t)
    return (
        out.reshape(kv_count, head_size, seq_rows, group_size)
        .transpose(2, 0, 3, 1)
        .reshape(1, seq_rows, head_count, head_size)
    )


def local(
    stream,
    queries,
    key_rows,
    value_rows,
    expert_ids,
    norm_gain,
    router_weight,
    gate_weight,
    up_weight,
    down_weight,
):
    ctx_count = lax.axis_size("ctx")
    exp_count = lax.axis_size("exp")
    tokens = stream.shape[1]
    features = stream.shape[2]
    top_count = expert_ids.shape[2]
    expert_total = router_weight.shape[1]
    per_ctx = expert_total // ctx_count
    quarters = exp_count // per_ctx
    capacity = 2 * tokens * top_count // expert_total

    attention_inputs = gather_attention_inputs(queries, key_rows, value_rows)
    stacked = jnp.stack([gate_weight, up_weight, down_weight], axis=0)
    across = from_partner(stacked, "exp", 2)
    own_beside = from_partner(stacked, "exp", 1)

    widened = stream[0].astype(jnp.float32)
    mean_square = jnp.mean(widened * widened, axis=-1, keepdims=True)
    normed = (widened * lax.rsqrt(mean_square + 1e-06) * norm_gain.astype(jnp.float32)).astype(
        jnp.bfloat16
    )
    logits = jnp.dot(normed, router_weight, preferred_element_type=jnp.float32)
    chosen = expert_ids[0]
    gate_values = jax.nn.sigmoid(jnp.take_along_axis(logits, chosen, axis=1))
    flat_ids = chosen.reshape(-1)
    onehot = (flat_ids[:, None] == jnp.arange(expert_total, dtype=jnp.int32)[None, :]).astype(
        jnp.int32
    )
    earlier = jnp.cumsum(onehot, axis=0) - onehot
    slot_index = jnp.sum(earlier * onehot, axis=1)
    target = flat_ids * capacity + slot_index
    tile_rows = 8
    tile = (tile_rows, features // tile_rows)
    source_rows = jnp.repeat(normed, top_count, axis=0)
    outgoing = (
        jnp.zeros((expert_total * capacity, features), jnp.bfloat16).at[target].set(source_rows)
    )
    outgoing = outgoing.reshape(-1, *tile)
    grid_axes = ("ctx", "exp")
    received = lax.all_to_all(outgoing, grid_axes, split_axis=0, concat_axis=0, tiled=True)
    across, received = lax.optimization_barrier((across, received))
    across_beside = from_partner(across, "exp", 1)
    held = jnp.concatenate([stacked, across, own_beside, across_beside], axis=1)
    received = received.reshape(-1, features)
    computed = expert_rows(received, held[0], held[1], held[2]).astype(jnp.bfloat16)
    computed = computed.reshape(-1, *tile)
    queries_held, computed = lax.optimization_barrier((attention_inputs[0], computed))
    attended = attention(queries_held, attention_inputs[1])
    came_back = lax.all_to_all(computed, grid_axes, split_axis=0, concat_axis=0, tiled=True)
    attended, came_back = lax.optimization_barrier((attended, came_back))
    flat_back = came_back.reshape(expert_total * capacity, features)
    picked = (
        jnp.take(flat_back, target, axis=0).astype(jnp.float32).reshape(tokens, top_count, features)
    )
    mixture = jnp.sum(picked * gate_values[:, :, None], axis=1).astype(jnp.bfloat16)
    return (attended, mixture[None])


def solution(mesh):
    placed = (
        P("exp", "ctx", None),
        P("exp", "ctx", None, None),
        P("exp", "ctx", None, None),
        P("exp", "ctx", None, None),
        P("exp", "ctx", None),
        P(),
        P(),
        P(("ctx", "exp"), None),
        P(("ctx", "exp"), None),
        P(("ctx", "exp"), None),
    )
    return jax.shard_map(
        local,
        mesh=mesh,
        in_specs=placed,
        out_specs=(P("exp", "ctx", None, None), P("exp", "ctx", None)),
        check_vma=False,
    )
```

```python
import functools
import math

import jax
import jax.numpy as jnp
from jax import lax
from jax.experimental import pallas as pl
from jax.experimental.pallas import tpu as pltpu
from jax.sharding import PartitionSpec as P


def from_partner(value, axis, flip):
    return lax.ppermute(value, axis, [(i, i ^ flip) for i in range(lax.axis_size(axis))])


def expert_rows(flat_rows, gate_rows, up_rows, down_rows):
    contract = (((1,), (1,)), ((), ()))
    gate_part = lax.dot_general(flat_rows, gate_rows, contract, preferred_element_type=jnp.float32)
    up_part = lax.dot_general(flat_rows, up_rows, contract, preferred_element_type=jnp.float32)
    hidden = (jax.nn.silu(gate_part) * up_part).astype(jnp.bfloat16)
    return jnp.dot(hidden, down_rows, preferred_element_type=jnp.float32)


def _flash_kernel(block, group, scaling, c_ref, qt_ref, k_ref, v_ref, o_ref, m_sc, l_sc, acc_sc):
    c = c_ref[0]
    qt = qt_ref[0]
    width = qt.shape[1]
    m_sc[...] = jnp.full(m_sc.shape, -1e30, jnp.float32)
    l_sc[...] = jnp.zeros(l_sc.shape, jnp.float32)
    acc_sc[...] = jnp.zeros(acc_sc.shape, jnp.float32)

    def update(j, masked, size=block):
        start = pl.multiple_of(j * size, size)
        k = k_ref[0, 0, pl.ds(start, size), :]
        v = v_ref[0, 0, pl.ds(start, size), :]
        s = jnp.dot(k, qt, preferred_element_type=jnp.float32) * scaling
        if masked:
            kpos = lax.broadcasted_iota(jnp.int32, (block, width), 0)
            qpos = lax.broadcasted_iota(jnp.int32, (block, width), 1) // group
            s = jnp.where(kpos <= qpos, s, -1e30)
        m_prev = m_sc[...]
        m_new = jnp.maximum(m_prev, jnp.max(s, axis=0, keepdims=True))
        alpha = jnp.exp(m_prev - m_new)
        p = jnp.exp(s - m_new)
        l_sc[...] = alpha * l_sc[...] + jnp.sum(p, axis=0, keepdims=True)
        acc_sc[...] = alpha * acc_sc[...] + lax.dot_general(
            v, p.astype(jnp.bfloat16), (((0,), (0,)), ((), ())), preferred_element_type=jnp.float32
        )
        m_sc[...] = m_new

    wide = 4 * block
    span = wide // block

    def body_wide(j, carry):
        update(j, False, wide)
        return carry

    def body(j, carry):
        update(j, False)
        return carry

    lax.fori_loop(0, c // span, body_wide, 0)
    lax.fori_loop(c // span * span, c, body, 0)
    update(c, True)
    o_ref[0] = (acc_sc[...] / l_sc[...]).astype(o_ref.dtype)


def gather_attention_inputs(queries, key_rows, value_rows):
    local_kv = jnp.stack([key_rows[0], value_rows[0]], axis=0).transpose(0, 2, 1, 3)
    gathered = lax.all_gather(local_kv, "ctx", axis=2, tiled=True)
    return queries, gathered


def attention(queries, gathered):
    seq_rows = queries.shape[1]
    head_count = queries.shape[2]
    head_size = queries.shape[3]
    kv_count = gathered.shape[1]
    group_size = head_count // kv_count
    scaling = 1.0 / math.sqrt(head_size)
    width = seq_rows * group_size
    grouped_t = (
        queries[0]
        .reshape(seq_rows, kv_count, group_size, head_size)
        .transpose(1, 3, 0, 2)
        .reshape(kv_count, head_size, width)
    )
    total_rows = gathered.shape[2]
    me = lax.axis_index("ctx").astype(jnp.int32).reshape(1)
    out = pl.pallas_call(
        functools.partial(_flash_kernel, seq_rows, group_size, scaling),
        grid_spec=pltpu.PrefetchScalarGridSpec(
            num_scalar_prefetch=1,
            grid=(kv_count,),
            in_specs=[
                pl.BlockSpec((1, head_size, width), lambda g, c: (g, 0, 0)),
                pl.BlockSpec((1, 1, total_rows, head_size), lambda g, c: (0, g, 0, 0)),
                pl.BlockSpec((1, 1, total_rows, head_size), lambda g, c: (1, g, 0, 0)),
            ],
            out_specs=pl.BlockSpec((1, head_size, width), lambda g, c: (g, 0, 0)),
            scratch_shapes=[
                pltpu.VMEM((1, width), jnp.float32),
                pltpu.VMEM((1, width), jnp.float32),
                pltpu.VMEM((head_size, width), jnp.float32),
            ],
        ),
        out_shape=jax.ShapeDtypeStruct((kv_count, head_size, width), jnp.bfloat16),
        cost_estimate=pl.CostEstimate(
            flops=2 * kv_count * width * total_rows * head_size,
            transcendentals=kv_count * width * total_rows // 2,
            bytes_accessed=4 * kv_count * total_rows * head_size + 4 * kv_count * width * head_size,
        ),
    )(me, grouped_t, gathered, gathered)
    return (
        out.reshape(kv_count, head_size, seq_rows, group_size)
        .transpose(2, 0, 3, 1)
        .reshape(1, seq_rows, head_count, head_size)
    )


def local(
    stream,
    queries,
    key_rows,
    value_rows,
    expert_ids,
    norm_gain,
    router_weight,
    gate_weight,
    up_weight,
    down_weight,
):
    ctx_count = lax.axis_size("ctx")
    exp_count = lax.axis_size("exp")
    tokens = stream.shape[1]
    features = stream.shape[2]
    top_count = expert_ids.shape[2]
    expert_total = router_weight.shape[1]
    per_ctx = expert_total // ctx_count
    quarters = exp_count // per_ctx
    capacity = 2 * tokens * top_count // expert_total

    attention_inputs = gather_attention_inputs(queries, key_rows, value_rows)
    stacked = jnp.stack([gate_weight, up_weight, down_weight], axis=0)
    across = from_partner(stacked, "exp", 2)
    own_beside = from_partner(stacked, "exp", 1)

    widened = stream[0].astype(jnp.float32)
    mean_square = jnp.mean(widened * widened, axis=-1, keepdims=True)
    normed = (widened * lax.rsqrt(mean_square + 1e-06) * norm_gain.astype(jnp.float32)).astype(
        jnp.bfloat16
    )
    logits = jnp.dot(normed, router_weight, preferred_element_type=jnp.float32)
    chosen = expert_ids[0]
    gate_values = jax.nn.sigmoid(jnp.take_along_axis(logits, chosen, axis=1))
    flat_ids = chosen.reshape(-1)
    onehot = (flat_ids[:, None] == jnp.arange(expert_total, dtype=jnp.int32)[None, :]).astype(
        jnp.int32
    )
    earlier = jnp.cumsum(onehot, axis=0) - onehot
    slot_index = jnp.sum(earlier * onehot, axis=1)
    target = flat_ids * capacity + slot_index
    tile_rows = 8
    tile = (tile_rows, features // tile_rows)
    source_rows = jnp.repeat(normed, top_count, axis=0)
    outgoing = (
        jnp.zeros((expert_total * capacity, features), jnp.bfloat16).at[target].set(source_rows)
    )
    outgoing = outgoing.reshape(-1, *tile)
    grid_axes = ("ctx", "exp")
    received = lax.all_to_all(outgoing, grid_axes, split_axis=0, concat_axis=0, tiled=True)
    across, received = lax.optimization_barrier((across, received))
    across_beside = from_partner(across, "exp", 1)
    held = jnp.concatenate([stacked, across, own_beside, across_beside], axis=1)
    received = received.reshape(-1, features)
    computed = expert_rows(received, held[0], held[1], held[2]).astype(jnp.bfloat16)
    computed = computed.reshape(-1, *tile)
    queries_held, computed = lax.optimization_barrier((attention_inputs[0], computed))
    attended = attention(queries_held, attention_inputs[1])
    came_back = lax.all_to_all(computed, grid_axes, split_axis=0, concat_axis=0, tiled=True)
    attended, came_back = lax.optimization_barrier((attended, came_back))
    flat_back = came_back.reshape(expert_total * capacity, features)
    picked = (
        jnp.take(flat_back, target, axis=0).astype(jnp.float32).reshape(tokens, top_count, features)
    )
    mixture = jnp.sum(picked * gate_values[:, :, None], axis=1).astype(jnp.bfloat16)
    return (attended, mixture[None])


def solution(mesh):
    placed = (
        P("exp", "ctx", None),
        P("exp", "ctx", None, None),
        P("exp", "ctx", None, None),
        P("exp", "ctx", None, None),
        P("exp", "ctx", None),
        P(),
        P(),
        P(("ctx", "exp"), None),
        P(("ctx", "exp"), None),
        P(("ctx", "exp"), None),
    )
    return jax.shard_map(
        local,
        mesh=mesh,
        in_specs=placed,
        out_specs=(P("exp", "ctx", None, None), P("exp", "ctx", None)),
        check_vma=False,
    )
```

```python
import functools
import math

import jax
import jax.numpy as jnp
from jax import lax
from jax.experimental import pallas as pl
from jax.experimental.pallas import tpu as pltpu
from jax.sharding import PartitionSpec as P


def from_partner(value, axis, flip):
    return lax.ppermute(value, axis, [(i, i ^ flip) for i in range(lax.axis_size(axis))])


def expert_rows(flat_rows, gate_rows, up_rows, down_rows):
    contract = (((1,), (1,)), ((), ()))
    gate_part = lax.dot_general(flat_rows, gate_rows, contract, preferred_element_type=jnp.float32)
    up_part = lax.dot_general(flat_rows, up_rows, contract, preferred_element_type=jnp.float32)
    hidden = (jax.nn.silu(gate_part) * up_part).astype(jnp.bfloat16)
    return jnp.dot(hidden, down_rows, preferred_element_type=jnp.float32)


def _flash_kernel(block, group, scaling, c_ref, qt_ref, k_ref, v_ref, o_ref, m_sc, l_sc, acc_sc):
    c = c_ref[0]
    qt = qt_ref[0]
    width = qt.shape[1]
    m_sc[...] = jnp.full(m_sc.shape, -1e30, jnp.float32)
    l_sc[...] = jnp.zeros(l_sc.shape, jnp.float32)
    acc_sc[...] = jnp.zeros(acc_sc.shape, jnp.float32)

    def update(j, masked, size=block):
        start = pl.multiple_of(j * size, size)
        k = k_ref[0, 0, pl.ds(start, size), :]
        v = v_ref[0, 0, pl.ds(start, size), :]
        s = jnp.dot(k, qt, preferred_element_type=jnp.float32) * scaling
        if masked:
            kpos = lax.broadcasted_iota(jnp.int32, (block, width), 0)
            qpos = lax.broadcasted_iota(jnp.int32, (block, width), 1) // group
            s = jnp.where(kpos <= qpos, s, -1e30)
        m_prev = m_sc[...]
        m_new = jnp.maximum(m_prev, jnp.max(s, axis=0, keepdims=True))
        alpha = jnp.exp(m_prev - m_new)
        p = jnp.exp(s - m_new)
        l_sc[...] = alpha * l_sc[...] + jnp.sum(p, axis=0, keepdims=True)
        acc_sc[...] = alpha * acc_sc[...] + lax.dot_general(
            v, p.astype(jnp.bfloat16), (((0,), (0,)), ((), ())), preferred_element_type=jnp.float32
        )
        m_sc[...] = m_new

    wide = 8 * block
    span = wide // block

    def body_wide(j, carry):
        update(j, False, wide)
        return carry

    def body(j, carry):
        update(j, False)
        return carry

    lax.fori_loop(0, c // span, body_wide, 0)
    lax.fori_loop(c // span * span, c, body, 0)
    update(c, True)
    o_ref[0] = (acc_sc[...] / l_sc[...]).astype(o_ref.dtype)


def gather_attention_inputs(queries, key_rows, value_rows):
    local_kv = jnp.stack([key_rows[0], value_rows[0]], axis=0).transpose(0, 2, 1, 3)
    gathered = lax.all_gather(local_kv, "ctx", axis=2, tiled=True)
    return queries, gathered


def attention(queries, gathered):
    seq_rows = queries.shape[1]
    head_count = queries.shape[2]
    head_size = queries.shape[3]
    kv_count = gathered.shape[1]
    group_size = head_count // kv_count
    scaling = 1.0 / math.sqrt(head_size)
    width = seq_rows * group_size
    grouped_t = (
        queries[0]
        .reshape(seq_rows, kv_count, group_size, head_size)
        .transpose(1, 3, 0, 2)
        .reshape(kv_count, head_size, width)
    )
    total_rows = gathered.shape[2]
    me = lax.axis_index("ctx").astype(jnp.int32).reshape(1)
    out = pl.pallas_call(
        functools.partial(_flash_kernel, seq_rows, group_size, scaling),
        grid_spec=pltpu.PrefetchScalarGridSpec(
            num_scalar_prefetch=1,
            grid=(kv_count,),
            in_specs=[
                pl.BlockSpec((1, head_size, width), lambda g, c: (g, 0, 0)),
                pl.BlockSpec((1, 1, total_rows, head_size), lambda g, c: (0, g, 0, 0)),
                pl.BlockSpec((1, 1, total_rows, head_size), lambda g, c: (1, g, 0, 0)),
            ],
            out_specs=pl.BlockSpec((1, head_size, width), lambda g, c: (g, 0, 0)),
            scratch_shapes=[
                pltpu.VMEM((1, width), jnp.float32),
                pltpu.VMEM((1, width), jnp.float32),
                pltpu.VMEM((head_size, width), jnp.float32),
            ],
        ),
        out_shape=jax.ShapeDtypeStruct((kv_count, head_size, width), jnp.bfloat16),
        cost_estimate=pl.CostEstimate(
            flops=2 * kv_count * width * total_rows * head_size,
            transcendentals=kv_count * width * total_rows // 2,
            bytes_accessed=4 * kv_count * total_rows * head_size + 4 * kv_count * width * head_size,
        ),
    )(me, grouped_t, gathered, gathered)
    return (
        out.reshape(kv_count, head_size, seq_rows, group_size)
        .transpose(2, 0, 3, 1)
        .reshape(1, seq_rows, head_count, head_size)
    )


def local(
    stream,
    queries,
    key_rows,
    value_rows,
    expert_ids,
    norm_gain,
    router_weight,
    gate_weight,
    up_weight,
    down_weight,
):
    ctx_count = lax.axis_size("ctx")
    exp_count = lax.axis_size("exp")
    tokens = stream.shape[1]
    features = stream.shape[2]
    top_count = expert_ids.shape[2]
    expert_total = router_weight.shape[1]
    per_ctx = expert_total // ctx_count
    quarters = exp_count // per_ctx
    capacity = 2 * tokens * top_count // expert_total

    attention_inputs = gather_attention_inputs(queries, key_rows, value_rows)
    stacked = jnp.stack([gate_weight, up_weight, down_weight], axis=0)
    across = from_partner(stacked, "exp", 2)
    own_beside = from_partner(stacked, "exp", 1)

    widened = stream[0].astype(jnp.float32)
    mean_square = jnp.mean(widened * widened, axis=-1, keepdims=True)
    normed = (widened * lax.rsqrt(mean_square + 1e-06) * norm_gain.astype(jnp.float32)).astype(
        jnp.bfloat16
    )
    logits = jnp.dot(normed, router_weight, preferred_element_type=jnp.float32)
    chosen = expert_ids[0]
    gate_values = jax.nn.sigmoid(jnp.take_along_axis(logits, chosen, axis=1))
    flat_ids = chosen.reshape(-1)
    onehot = (flat_ids[:, None] == jnp.arange(expert_total, dtype=jnp.int32)[None, :]).astype(
        jnp.int32
    )
    earlier = jnp.cumsum(onehot, axis=0) - onehot
    slot_index = jnp.sum(earlier * onehot, axis=1)
    target = flat_ids * capacity + slot_index
    tile_rows = 8
    tile = (tile_rows, features // tile_rows)
    source_rows = jnp.repeat(normed, top_count, axis=0)
    outgoing = (
        jnp.zeros((expert_total * capacity, features), jnp.bfloat16).at[target].set(source_rows)
    )
    outgoing = outgoing.reshape(-1, *tile)
    grid_axes = ("ctx", "exp")
    received = lax.all_to_all(outgoing, grid_axes, split_axis=0, concat_axis=0, tiled=True)
    across, received = lax.optimization_barrier((across, received))
    across_beside = from_partner(across, "exp", 1)
    held = jnp.concatenate([stacked, across, own_beside, across_beside], axis=1)
    received = received.reshape(-1, features)
    computed = expert_rows(received, held[0], held[1], held[2]).astype(jnp.bfloat16)
    computed = computed.reshape(-1, *tile)
    queries_held, computed = lax.optimization_barrier((attention_inputs[0], computed))
    attended = attention(queries_held, attention_inputs[1])
    came_back = lax.all_to_all(computed, grid_axes, split_axis=0, concat_axis=0, tiled=True)
    attended, came_back = lax.optimization_barrier((attended, came_back))
    flat_back = came_back.reshape(expert_total * capacity, features)
    picked = (
        jnp.take(flat_back, target, axis=0).astype(jnp.float32).reshape(tokens, top_count, features)
    )
    mixture = jnp.sum(picked * gate_values[:, :, None], axis=1).astype(jnp.bfloat16)
    return (attended, mixture[None])


def solution(mesh):
    placed = (
        P("exp", "ctx", None),
        P("exp", "ctx", None, None),
        P("exp", "ctx", None, None),
        P("exp", "ctx", None, None),
        P("exp", "ctx", None),
        P(),
        P(),
        P(("ctx", "exp"), None),
        P(("ctx", "exp"), None),
        P(("ctx", "exp"), None),
    )
    return jax.shard_map(
        local,
        mesh=mesh,
        in_specs=placed,
        out_specs=(P("exp", "ctx", None, None), P("exp", "ctx", None)),
        check_vma=False,
    )
```

```python
import functools
import math

import jax
import jax.numpy as jnp
from jax import lax
from jax.experimental import pallas as pl
from jax.experimental.pallas import tpu as pltpu
from jax.sharding import PartitionSpec as P


def from_partner(value, axis, flip):
    return lax.ppermute(value, axis, [(i, i ^ flip) for i in range(lax.axis_size(axis))])


def expert_rows(flat_rows, gate_rows, up_rows, down_rows):
    contract = (((1,), (1,)), ((), ()))
    gate_part = lax.dot_general(flat_rows, gate_rows, contract, preferred_element_type=jnp.float32)
    up_part = lax.dot_general(flat_rows, up_rows, contract, preferred_element_type=jnp.float32)
    hidden = (jax.nn.silu(gate_part) * up_part).astype(jnp.bfloat16)
    return jnp.dot(hidden, down_rows, preferred_element_type=jnp.float32)


def _flash_kernel(block, group, scaling, c_ref, qt_ref, k_ref, v_ref, o_ref, m_sc, l_sc, acc_sc):
    c = c_ref[0]
    qt = qt_ref[0]
    width = qt.shape[1]
    m_sc[...] = jnp.full(m_sc.shape, -1e30, jnp.float32)
    l_sc[...] = jnp.zeros(l_sc.shape, jnp.float32)
    acc_sc[...] = jnp.zeros(acc_sc.shape, jnp.float32)

    def update(j, masked, size=block):
        start = pl.multiple_of(j * size, size)
        k = k_ref[0, 0, pl.ds(start, size), :]
        v = v_ref[0, 0, pl.ds(start, size), :]
        s = jnp.dot(k, qt, preferred_element_type=jnp.float32) * scaling
        if masked:
            kpos = lax.broadcasted_iota(jnp.int32, (block, width), 0)
            qpos = lax.broadcasted_iota(jnp.int32, (block, width), 1) // group
            s = jnp.where(kpos <= qpos, s, -1e30)
        m_prev = m_sc[...]
        m_new = jnp.maximum(m_prev, jnp.max(s, axis=0, keepdims=True))
        alpha = jnp.exp(m_prev - m_new)
        p = jnp.exp(s - m_new)
        l_sc[...] = alpha * l_sc[...] + jnp.sum(p, axis=0, keepdims=True)
        acc_sc[...] = alpha * acc_sc[...] + lax.dot_general(
            v, p.astype(jnp.bfloat16), (((0,), (0,)), ((), ())), preferred_element_type=jnp.float32
        )
        m_sc[...] = m_new

    wide = 4 * block
    span = wide // block

    def body_wide(j, carry):
        update(j, False, wide)
        return carry

    def body(j, carry):
        update(j, False)
        return carry

    lax.fori_loop(0, c // span, body_wide, 0)
    lax.fori_loop(c // span * span, c, body, 0)
    update(c, True)
    result = (acc_sc[...] / l_sc[...]).T
    o_ref[...] = result.reshape(o_ref.shape).astype(o_ref.dtype)


def gather_attention_inputs(queries, key_rows, value_rows):
    local_kv = jnp.stack([key_rows[0], value_rows[0]], axis=0).transpose(0, 2, 1, 3)
    gathered = lax.all_gather(local_kv, "ctx", axis=2, tiled=True)
    return queries, gathered


def attention(queries, gathered):
    seq_rows = queries.shape[1]
    head_count = queries.shape[2]
    head_size = queries.shape[3]
    kv_count = gathered.shape[1]
    group_size = head_count // kv_count
    scaling = 1.0 / math.sqrt(head_size)
    width = seq_rows * group_size
    grouped_t = (
        queries[0]
        .reshape(seq_rows, kv_count, group_size, head_size)
        .transpose(1, 3, 0, 2)
        .reshape(kv_count, head_size, width)
    )
    total_rows = gathered.shape[2]
    me = lax.axis_index("ctx").astype(jnp.int32).reshape(1)
    out = pl.pallas_call(
        functools.partial(_flash_kernel, seq_rows, group_size, scaling),
        grid_spec=pltpu.PrefetchScalarGridSpec(
            num_scalar_prefetch=1,
            grid=(kv_count,),
            in_specs=[
                pl.BlockSpec((1, head_size, width), lambda g, c: (g, 0, 0)),
                pl.BlockSpec((1, 1, total_rows, head_size), lambda g, c: (0, g, 0, 0)),
                pl.BlockSpec((1, 1, total_rows, head_size), lambda g, c: (1, g, 0, 0)),
            ],
            out_specs=pl.BlockSpec((seq_rows, group_size, head_size), lambda g, c: (0, g, 0)),
            scratch_shapes=[
                pltpu.VMEM((1, width), jnp.float32),
                pltpu.VMEM((1, width), jnp.float32),
                pltpu.VMEM((head_size, width), jnp.float32),
            ],
        ),
        out_shape=jax.ShapeDtypeStruct((seq_rows, head_count, head_size), jnp.bfloat16),
        cost_estimate=pl.CostEstimate(
            flops=2 * kv_count * width * total_rows * head_size,
            transcendentals=kv_count * width * total_rows // 2,
            bytes_accessed=4 * kv_count * total_rows * head_size + 4 * kv_count * width * head_size,
        ),
    )(me, grouped_t, gathered, gathered)
    return out[None]


def local(
    stream,
    queries,
    key_rows,
    value_rows,
    expert_ids,
    norm_gain,
    router_weight,
    gate_weight,
    up_weight,
    down_weight,
):
    ctx_count = lax.axis_size("ctx")
    exp_count = lax.axis_size("exp")
    tokens = stream.shape[1]
    features = stream.shape[2]
    top_count = expert_ids.shape[2]
    expert_total = router_weight.shape[1]
    per_ctx = expert_total // ctx_count
    quarters = exp_count // per_ctx
    capacity = 2 * tokens * top_count // expert_total

    attention_inputs = gather_attention_inputs(queries, key_rows, value_rows)
    stacked = jnp.stack([gate_weight, up_weight, down_weight], axis=0)
    across = from_partner(stacked, "exp", 2)
    own_beside = from_partner(stacked, "exp", 1)

    widened = stream[0].astype(jnp.float32)
    mean_square = jnp.mean(widened * widened, axis=-1, keepdims=True)
    normed = (widened * lax.rsqrt(mean_square + 1e-06) * norm_gain.astype(jnp.float32)).astype(
        jnp.bfloat16
    )
    logits = jnp.dot(normed, router_weight, preferred_element_type=jnp.float32)
    chosen = expert_ids[0]
    gate_values = jax.nn.sigmoid(jnp.take_along_axis(logits, chosen, axis=1))
    flat_ids = chosen.reshape(-1)
    onehot = (flat_ids[:, None] == jnp.arange(expert_total, dtype=jnp.int32)[None, :]).astype(
        jnp.int32
    )
    earlier = jnp.cumsum(onehot, axis=0) - onehot
    slot_index = jnp.sum(earlier * onehot, axis=1)
    target = flat_ids * capacity + slot_index
    tile_rows = 8
    tile = (tile_rows, features // tile_rows)
    source_rows = jnp.repeat(normed, top_count, axis=0)
    outgoing = (
        jnp.zeros((expert_total * capacity, features), jnp.bfloat16).at[target].set(source_rows)
    )
    outgoing = outgoing.reshape(-1, *tile)
    grid_axes = ("ctx", "exp")
    received = lax.all_to_all(outgoing, grid_axes, split_axis=0, concat_axis=0, tiled=True)
    across, received = lax.optimization_barrier((across, received))
    across_beside = from_partner(across, "exp", 1)
    held = jnp.concatenate([stacked, across, own_beside, across_beside], axis=1)
    received = received.reshape(-1, features)
    computed = expert_rows(received, held[0], held[1], held[2]).astype(jnp.bfloat16)
    computed = computed.reshape(-1, *tile)
    queries_held, computed = lax.optimization_barrier((attention_inputs[0], computed))
    attended = attention(queries_held, attention_inputs[1])
    came_back = lax.all_to_all(computed, grid_axes, split_axis=0, concat_axis=0, tiled=True)
    attended, came_back = lax.optimization_barrier((attended, came_back))
    flat_back = came_back.reshape(expert_total * capacity, features)
    picked = (
        jnp.take(flat_back, target, axis=0).astype(jnp.float32).reshape(tokens, top_count, features)
    )
    mixture = jnp.sum(picked * gate_values[:, :, None], axis=1).astype(jnp.bfloat16)
    return (attended, mixture[None])


def solution(mesh):
    placed = (
        P("exp", "ctx", None),
        P("exp", "ctx", None, None),
        P("exp", "ctx", None, None),
        P("exp", "ctx", None, None),
        P("exp", "ctx", None),
        P(),
        P(),
        P(("ctx", "exp"), None),
        P(("ctx", "exp"), None),
        P(("ctx", "exp"), None),
    )
    return jax.shard_map(
        local,
        mesh=mesh,
        in_specs=placed,
        out_specs=(P("exp", "ctx", None, None), P("exp", "ctx", None)),
        check_vma=False,
    )
```
